256 devices in a mesh: space: 32 (over z_lo, x, core), group: 8 (over y, z_hi).
Axes of the slice: x: 4, y: 4, z: 8 (z_hi: 2, z_lo: 4; z = z_hi * 4 + z_lo), core: 2. Of those that a mesh axis runs over, the one named last changes fastest.
Arguments:
- features: bfloat16 [8, 2048, 2432], P('group', 'space'), may hold values from -6 to 6
- positions: float32 [8, 3, 2048], P('group', None, 'space'), may hold values from 0 to 12
- cell_box: float32 [8, 3], P('group'), may hold values from 10 to 14
- send_rows: int32 [8, 2048], P('group', 'space'), may hold values from 0 to 63
- neighbours: int32 [8, 2048, 2], P('group', 'space'), may hold values from 0 to 127
- edge_mask: int32 [8, 2048, 2], P('group', 'space'), may hold values 0 or 1
- shift_ids: int32 [8, 2048, 2], P('group', 'space'), may hold values from 0 to 26
- target_forces: float32 [8, 3, 2048], P('group', None, 'space'), may hold values from -64 to 64
- w_zero: bfloat16 [896, 896], replicated, may hold values from -0.1875 to 0.1875
- w_real: bfloat16 [768, 768], replicated, may hold values from -0.15625 to 0.15625
- w_imag: bfloat16 [768, 768], replicated, may hold values from -0.15625 to 0.15625
- radial: float32 [600, 128], replicated, may hold values from -4 to 4
- readout: float32 [128], replicated, may hold values from -0.5 to 0.5
Outputs:
- forces: float32 [8, 3, 2048], P('group', None, 'space')
- grad_zero: float32 [896, 896], replicated
- grad_real: float32 [768, 768], replicated
- grad_imag: float32 [768, 768], replicated
- grad_radial: float32 [600, 128], replicated
- grad_readout: float32 [128], replicated
The draws below stay inside these ranges and needn't reach their ends.
Inputs may be any that keep to these rules, and one draw needn't show every extreme that they name: `send_rows`: rows of the sending partition's own atoms. `neighbours`: rows of the partition's table of 128 atoms.
All inputs are finite; a program needn't handle non-finite values. No bound on the sum of `edge_mask` on one device may be relied on, other than what follows from the above.
Results may differ from the reference program's by a relative error of at most 0.0154.
Values may be sent and summed in bfloat16 or wider, within the bound.
No kernel may reach another device: no remote copies, remote signals or barrier semaphores. Data moves between devices by JAX's collectives and lax.ppermute only.
A program may use at most 128 MiB of HBM per device.

```python
import math
import jax
import jax.numpy as jnp
from jax import lax

C = 128
COEFS = 19
NB = 600
DEG = 2
A_DEV = 64
GHOSTS = 32
ATOMS = 2048
N_SPACE = 32
N_GROUP = 8


def draw_target_forces(key, part):
    first_key = jax.random.fold_in(key, 11)
    second_key = jax.random.fold_in(key, 23)
    base = 0.5 * jax.random.truncated_normal(first_key, -4.0, 4.0, (N_GROUP, 3, N_SPACE, A_DEV), jnp.float32)
    logs = jax.random.uniform(second_key, (N_GROUP, 1, N_SPACE, 1), jnp.float32, 0.0, math.log(16.0))
    heavy = (jnp.arange(N_SPACE) == N_SPACE // 2 - 1)[None, None, :, None]
    scale = jnp.where(heavy, 16.0, jnp.exp(logs))
    values = jnp.clip(base * scale, -64.0, 64.0)
    return values.reshape(N_GROUP, 3, N_SPACE * A_DEV).astype(jnp.float32)


def place_ends(drawn, key, low, top_value):
    spot = [jax.random.randint(jax.random.fold_in(key, axis), (), 0, length) for axis, length in enumerate(drawn.shape)]
    widest = drawn.shape.index(max(drawn.shape))
    neighbour = spot[:widest] + [(spot[widest] + 1) % drawn.shape[widest]] + spot[widest + 1:]
    return drawn.at[tuple(spot)].set(low).at[tuple(neighbour)].set(top_value)


def shard_levels(key, extent, cuts, least, high):
    def one(dim, blocks):
        steps = jax.random.uniform(jax.random.fold_in(jax.random.fold_in(key, 6), dim), (blocks,), jnp.float32, least / len(cuts), high / len(cuts))
        return jnp.repeat(jnp.exp(steps), extent[dim] // blocks).reshape((-1,) + (1,) * (len(extent) - dim - 1))

    loudness = one(*cuts[0])
    for cut in cuts[1:]:
        loudness = loudness * one(*cut)
    return loudness


def scatter_about(own_key, dims, deviation, most, shards=(), held_as=jnp.bfloat16):
    drawn = deviation * jax.random.normal(own_key, dims, jnp.float32)
    if shards:
        drawn = drawn * shard_levels(own_key, dims, shards, -0.22, 0.18)
    return jnp.clip(drawn, -most, most).astype(held_as)


def setup_inputs(seed: int = 0) -> dict:
    key_of = jax.random.split(jax.random.key(seed), 14)
    return {
        "features": scatter_about(key_of[0], (N_GROUP, ATOMS, COEFS * C), 1.0, 6.0, ((0, 8), (1, 32))),
        "positions": jnp.clip(12.0 * jax.random.uniform(key_of[1], (N_GROUP, 3, ATOMS), jnp.float32) ** shard_levels(key_of[1], (N_GROUP, 3, ATOMS), ((0, 8), (2, 32)), -0.2, 0.2), 0.0, 12.0),
        "cell_box": jnp.clip(10.0 + 4.0 * jax.random.uniform(key_of[2], (N_GROUP, 3), jnp.float32) ** shard_levels(key_of[2], (N_GROUP, 3), ((0, 8),), -0.2, 0.2), 10.0, 14.0),
        "send_rows": place_ends(jax.random.randint(key_of[3], (N_GROUP, N_SPACE * 2 * GHOSTS), 0, A_DEV), jax.random.fold_in(key_of[3], 1), 0, A_DEV - 1).astype(jnp.int32),
        "neighbours": place_ends(jax.random.randint(key_of[4], (N_GROUP, ATOMS, DEG), 0, A_DEV + 2 * GHOSTS), jax.random.fold_in(key_of[4], 1), 0, (A_DEV + 2 * GHOSTS) - 1).astype(jnp.int32),
        "edge_mask": place_ends((jax.random.randint(key_of[5], (N_GROUP, ATOMS, DEG), 0, 4) < 3).astype(jnp.int32), jax.random.fold_in(key_of[5], 1), 0, 1),
        "shift_ids": place_ends(jax.random.randint(key_of[6], (N_GROUP, ATOMS, DEG), 0, 27), jax.random.fold_in(key_of[6], 1), 0, 26).astype(jnp.int32),
        "target_forces": draw_target_forces(jax.random.fold_in(key_of[13], 71), 0),
        "w_zero": scatter_about(key_of[8], (7 * C, 7 * C), (7 * C) ** -0.5, 0.1875),
        "w_real": scatter_about(key_of[9], (6 * C, 6 * C), (12 * C) ** -0.5, 0.15625),
        "w_imag": scatter_about(key_of[10], (6 * C, 6 * C), (12 * C) ** -0.5, 0.15625),
        "radial": scatter_about(key_of[11], (NB, C), 0.8, 4.0, (), jnp.float32),
        "readout": scatter_about(key_of[12], (C,), C ** -0.5, 0.5, (), jnp.float32),
    }


RANGE_TOP = 48.0

def energy(params, table_feats, table_pos, neighbours, edge_mask, shift_ids, cell_box):
    w_zero, w_real, w_imag, radial, readout = params
    target_count, degree = neighbours.shape
    levels, channels = radial.shape
    flat_ids = neighbours.reshape(-1)
    edges = flat_ids.shape[0]
    shift_list = shift_ids.reshape(-1)
    offset = jnp.stack([shift_list // 9 - 1, shift_list // 3 % 3 - 1, shift_list % 3 - 1]).astype(jnp.float32) * cell_box[:, None]
    edge_vec = jnp.take(table_pos, flat_ids, axis=1) + offset - jnp.repeat(table_pos[:, :target_count], degree, axis=1)
    delta_one, delta_two, delta_three = (edge_vec[0], edge_vec[1], edge_vec[2])
    planar = jnp.sqrt(delta_one * delta_one + delta_two * delta_two + 1.0)
    radius = jnp.sqrt(planar * planar + delta_three * delta_three)
    cos_phi = (delta_one / planar)[:, None, None]
    sin_phi = (delta_two / planar)[:, None, None]
    cos_tilt = (delta_three / radius)[:, None, None]
    sin_tilt = (planar / radius)[:, None, None]
    spacing = RANGE_TOP / (levels - 1)
    centers = jnp.arange(levels, dtype=jnp.float32) * spacing
    basis_vals = jnp.exp(-jnp.square((radius[:, None] - centers[None, :]) / (2.0 * spacing)))
    radial_gain = jnp.dot(basis_vals, radial, precision=lax.Precision.HIGHEST)[:, None, :]
    source = jnp.take(table_feats, flat_ids, axis=0).astype(jnp.float32).reshape(edges, 19, channels)
    zero_part = source[:, 0:7]
    plus_part = source[:, 7:13]
    minus_part = source[:, 13:19]
    plus_turn = cos_phi * plus_part + sin_phi * minus_part
    minus_turn = cos_phi * minus_part - sin_phi * plus_part
    upper = zero_part[:, 1:]
    upper_tilt = cos_tilt * upper - sin_tilt * plus_turn
    plus_tilt = sin_tilt * upper + cos_tilt * plus_turn
    in_zero = (jnp.concatenate([zero_part[:, 0:1], upper_tilt], 1) * radial_gain).reshape(edges, 7 * channels).astype(jnp.bfloat16)
    in_plus = (plus_tilt * radial_gain).reshape(edges, 6 * channels).astype(jnp.bfloat16)
    in_minus = (minus_turn * radial_gain).reshape(edges, 6 * channels).astype(jnp.bfloat16)
    weight_zero = w_zero.astype(jnp.bfloat16)
    weight_real = w_real.astype(jnp.bfloat16)
    weight_imag = w_imag.astype(jnp.bfloat16)
    out_zero = jnp.dot(in_zero, weight_zero, preferred_element_type=jnp.float32).reshape(edges, 7, channels)
    out_plus = (jnp.dot(in_plus, weight_real, preferred_element_type=jnp.float32) - jnp.dot(in_minus, weight_imag, preferred_element_type=jnp.float32)).reshape(edges, 6, channels)
    out_minus = (jnp.dot(in_plus, weight_imag, preferred_element_type=jnp.float32) + jnp.dot(in_minus, weight_real, preferred_element_type=jnp.float32)).reshape(edges, 6, channels)
    upper_back = cos_tilt * out_zero[:, 1:] + sin_tilt * out_plus
    plus_back = cos_tilt * out_plus - sin_tilt * out_zero[:, 1:]
    plus_final = cos_phi * plus_back - sin_phi * out_minus
    minus_final = cos_phi * out_minus + sin_phi * plus_back
    message = jnp.concatenate([out_zero[:, 0:1], upper_back, plus_final, minus_final], 1)
    message = message * edge_mask.reshape(-1).astype(jnp.float32)[:, None, None]
    summed = message.reshape(target_count, degree, 19, channels).sum(axis=1) / degree
    updated = table_feats[:target_count].astype(jnp.float32).reshape(target_count, 19, channels) + summed
    invariant = updated[:, 0, :] + lax.optimization_barrier(jnp.mean(updated * updated, axis=1))
    return jnp.sum(jax.nn.silu(invariant) * readout[None, :])

def partition_rows(send_cell, part):
    ghosts = send_cell.shape[1] // 2
    below = (part + N_SPACE - 1) % N_SPACE
    above = (part + 1) % N_SPACE
    own_rows = part * A_DEV + jnp.arange(A_DEV, dtype=jnp.int32)
    below_rows = below * A_DEV + send_cell[below, ghosts:]
    above_rows = above * A_DEV + send_cell[above, :ghosts]
    return jnp.concatenate([own_rows.astype(jnp.int32), below_rows.astype(jnp.int32), above_rows.astype(jnp.int32)])

def reference(features, positions, cell_box, send_rows, neighbours, edge_mask, shift_ids, target_forces, w_zero, w_real, w_imag, radial, readout):
    params = (w_zero.astype(jnp.float32), w_real.astype(jnp.float32), w_imag.astype(jnp.float32), radial, readout)
    ghosts = send_rows.shape[1] // (2 * N_SPACE)
    part_ids = jnp.arange(N_SPACE, dtype=jnp.int32)

    def one_cell(totals, cell):
        atom_feats, atom_pos, box_sides, sends, neighbour_ids, edge_live, shift_list, wanted = cell
        send_cell = sends.reshape(N_SPACE, 2 * ghosts)
        neighbour_parts = neighbour_ids.reshape(N_SPACE, A_DEV, -1)
        live_parts = edge_live.reshape(N_SPACE, A_DEV, -1)
        shift_parts = shift_list.reshape(N_SPACE, A_DEV, -1)

        def position_grad(weights, part):
            table_rows = partition_rows(send_cell, part)
            table_feats = jnp.take(atom_feats, table_rows, axis=0)
            table_pos = jnp.take(atom_pos, table_rows, axis=1)
            return jax.grad(energy, 2)(weights, table_feats, table_pos, neighbour_parts[part], live_parts[part], shift_parts[part], box_sides)
        grad_tables = lax.map(lambda part: position_grad(params, part), part_ids)
        own_grad = grad_tables[:, :, :A_DEV]
        from_below = grad_tables[:, :, A_DEV:A_DEV + ghosts]
        from_above = grad_tables[:, :, A_DEV + ghosts:]
        returned = jnp.concatenate([jnp.roll(from_above, 1, axis=0), jnp.roll(from_below, -1, axis=0)], axis=2)
        onehot = (send_cell[:, :, None] == jnp.arange(A_DEV, dtype=jnp.int32)[None, None, :]).astype(jnp.float32)
        added = jnp.einsum('sxg,sga->sxa', returned, onehot, precision=lax.Precision.HIGHEST)
        part_forces = -(own_grad + added)
        forces = jnp.transpose(part_forces, (1, 0, 2)).reshape(3, N_SPACE * A_DEV)
        loss_weights = 2.0 * (forces - wanted) / (N_SPACE * A_DEV)

        def second_pass(carry, part):
            table_rows = partition_rows(send_cell, part)
            table_u = jnp.take(loss_weights, table_rows, axis=1)
            unused, pullback = jax.vjp(lambda weights: position_grad(weights, part), params)
            contrib, = pullback(-table_u)
            return (jax.tree.map(jnp.add, carry, contrib), None)
        totals, unused = lax.scan(second_pass, totals, part_ids)
        return (totals, forces)
    zeros = jax.tree.map(jnp.zeros_like, params)
    totals, forces = lax.scan(one_cell, zeros, (features, positions, cell_box, send_rows, neighbours, edge_mask, shift_ids, target_forces))
    return (forces, totals[0], totals[1], totals[2], totals[3], totals[4])
```

```python
import jax
import jax.numpy as jnp
from jax import lax
from jax.sharding import Mesh, PartitionSpec as P

RANGE_TOP = 48.0


def padded(cells, sides, width):
    for axis, dim in sides:
        count = lax.axis_size(axis)
        head = lax.slice_in_dim(cells, 0, width, axis=dim)
        tail = lax.slice_in_dim(cells, cells.shape[dim] - width, cells.shape[dim], axis=dim)
        cells = jnp.concatenate(
            [
                lax.ppermute(tail, axis, [(i, (i + 1) % count) for i in range(count)]),
                cells,
                lax.ppermute(head, axis, [((i + 1) % count, i) for i in range(count)]),
            ],
            axis=dim,
        )
    return cells


def energy(params, table_feats, table_pos, neighbours, edge_mask, shift_ids, cell_box):
    w_zero, w_real, w_imag, radial, readout = params
    target_count, degree = neighbours.shape
    levels, channels = radial.shape
    flat_ids = neighbours.reshape(-1)
    edges = flat_ids.shape[0]
    shift_list = shift_ids.reshape(-1)
    offset = (
        jnp.stack([shift_list // 9 - 1, shift_list // 3 % 3 - 1, shift_list % 3 - 1]).astype(
            jnp.float32
        )
        * cell_box[:, None]
    )
    edge_vec = (
        jnp.take(table_pos, flat_ids, axis=1)
        + offset
        - jnp.repeat(table_pos[:, :target_count], degree, axis=1)
    )
    delta_one, delta_two, delta_three = (edge_vec[0], edge_vec[1], edge_vec[2])
    planar = jnp.sqrt(delta_one * delta_one + delta_two * delta_two + 1.0)
    radius = jnp.sqrt(planar * planar + delta_three * delta_three)
    cos_phi = (delta_one / planar)[:, None, None]
    sin_phi = (delta_two / planar)[:, None, None]
    cos_tilt = (delta_three / radius)[:, None, None]
    sin_tilt = (planar / radius)[:, None, None]
    spacing = RANGE_TOP / (levels - 1)
    centers = jnp.arange(levels, dtype=jnp.float32) * spacing
    basis_vals = jnp.exp(-jnp.square((radius[:, None] - centers[None, :]) / (2.0 * spacing)))
    radial_gain = jnp.dot(basis_vals, radial, precision=lax.Precision.HIGHEST)[:, None, :]
    source = (
        jnp.take(table_feats, flat_ids, axis=0).astype(jnp.float32).reshape(edges, 19, channels)
    )
    zero_part = source[:, 0:7]
    plus_part = source[:, 7:13]
    minus_part = source[:, 13:19]
    plus_turn = cos_phi * plus_part + sin_phi * minus_part
    minus_turn = cos_phi * minus_part - sin_phi * plus_part
    upper = zero_part[:, 1:]
    upper_tilt = cos_tilt * upper - sin_tilt * plus_turn
    plus_tilt = sin_tilt * upper + cos_tilt * plus_turn
    in_zero = (
        (jnp.concatenate([zero_part[:, 0:1], upper_tilt], 1) * radial_gain)
        .reshape(edges, 7 * channels)
        .astype(jnp.bfloat16)
    )
    in_plus = (plus_tilt * radial_gain).reshape(edges, 6 * channels).astype(jnp.bfloat16)
    in_minus = (minus_turn * radial_gain).reshape(edges, 6 * channels).astype(jnp.bfloat16)
    weight_zero = w_zero.astype(jnp.bfloat16)
    weight_real = w_real.astype(jnp.bfloat16)
    weight_imag = w_imag.astype(jnp.bfloat16)
    out_zero = jnp.dot(in_zero, weight_zero, preferred_element_type=jnp.float32).reshape(
        edges, 7, channels
    )
    out_plus = (
        jnp.dot(in_plus, weight_real, preferred_element_type=jnp.float32)
        - jnp.dot(in_minus, weight_imag, preferred_element_type=jnp.float32)
    ).reshape(edges, 6, channels)
    out_minus = (
        jnp.dot(in_plus, weight_imag, preferred_element_type=jnp.float32)
        + jnp.dot(in_minus, weight_real, preferred_element_type=jnp.float32)
    ).reshape(edges, 6, channels)
    upper_back = cos_tilt * out_zero[:, 1:] + sin_tilt * out_plus
    plus_back = cos_tilt * out_plus - sin_tilt * out_zero[:, 1:]
    plus_final = cos_phi * plus_back - sin_phi * out_minus
    minus_final = cos_phi * out_minus + sin_phi * plus_back
    message = jnp.concatenate([out_zero[:, 0:1], upper_back, plus_final, minus_final], 1)
    message = message * edge_mask.reshape(-1).astype(jnp.float32)[:, None, None]
    summed = message.reshape(target_count, degree, 19, channels).sum(axis=1) / degree
    updated = (
        table_feats[:target_count].astype(jnp.float32).reshape(target_count, 19, channels) + summed
    )
    invariant = updated[:, 0, :] + jnp.mean(updated * updated, axis=1)
    return jnp.sum(jax.nn.silu(invariant) * readout[None, :])


def per_device(
    features,
    positions,
    cell_box,
    send_rows,
    neighbours,
    edge_mask,
    shift_ids,
    target_forces,
    w_zero,
    w_real,
    w_imag,
    radial,
    readout,
):
    atom_feats = features[0]
    atom_pos = positions[0]
    box_sides = cell_box[0]
    sends = send_rows[0]
    neighbour_ids = neighbours[0]
    edge_live = edge_mask[0]
    shift_list = shift_ids[0]
    wanted = target_forces[0]
    own_count = atom_feats.shape[0]
    ghosts = sends.shape[0] // 2
    part_count = lax.axis_size(SPACE)
    listed = jnp.take(atom_feats, sends, axis=0)
    beside_all = padded(listed, ((SPACE, 0),), ghosts)
    table_feats = jnp.concatenate([atom_feats, beside_all[:ghosts], beside_all[3 * ghosts :]], 0)
    spots = jnp.take(atom_pos, sends, axis=1)
    nearby = padded(spots, ((SPACE, 1),), ghosts)
    table_pos = jnp.concatenate([atom_pos, nearby[:, :ghosts], nearby[:, 3 * ghosts :]], 1)
    params = (
        w_zero.astype(jnp.float32),
        w_real.astype(jnp.float32),
        w_imag.astype(jnp.float32),
        radial,
        readout,
    )

    def position_grad(weights):
        return jax.grad(energy, 2)(
            weights, table_feats, table_pos, neighbour_ids, edge_live, shift_list, box_sides
        )

    grad_pos, pullback = jax.vjp(position_grad, params)
    ghost_grad = grad_pos[:, own_count:]
    backed = padded(ghost_grad, ((SPACE, 1),), ghosts)
    returned = jnp.concatenate([backed[:, :ghosts], backed[:, 3 * ghosts :]], 1)
    onehot = (sends[:, None] == jnp.arange(own_count, dtype=jnp.int32)[None, :]).astype(jnp.float32)
    added = jnp.dot(returned, onehot, precision=lax.Precision.HIGHEST)
    forces = -(grad_pos[:, :own_count] + added)
    loss_weights = 2.0 * (forces - wanted) / (part_count * own_count)
    picked = jnp.take(loss_weights, sends, axis=1)
    shared = padded(picked, ((SPACE, 1),), ghosts)
    table_u = jnp.concatenate([loss_weights, shared[:, :ghosts], shared[:, 3 * ghosts :]], 1)
    (grads,) = pullback(-table_u)
    grad_zero, grad_real, grad_imag, grad_radial, grad_readout = all_sum(grads)
    return (forces[None], grad_zero, grad_real, grad_imag, grad_radial, grad_readout)


SPACE = ("zl", "x", "c")
GROUP = ("y", "zh")
STAGES = (("c",), ("x", "y"), ("zh", "zl"))


def all_sum(grads):
    lanes = 128
    sizes = [g.size for g in grads]
    total = sum(sizes)
    devices = 1
    for stage in STAGES:
        devices *= lax.axis_size(stage)
    rows = -(-total // lanes)
    rows = -(-rows // (devices * 16)) * devices * 16
    flat = jnp.concatenate(
        [g.reshape(-1) for g in grads] + [jnp.zeros((rows * lanes - total,), jnp.float32)]
    )
    part = flat.astype(jnp.bfloat16).reshape(rows, lanes)
    for stage in STAGES:
        count = lax.axis_size(stage)
        got = lax.all_to_all(part, stage, 0, 0, tiled=True)
        part = got.reshape(count, -1, lanes).astype(jnp.float32).sum(0).astype(jnp.bfloat16)
    for stage in STAGES[::-1]:
        count = lax.axis_size(stage)
        spread = jnp.broadcast_to(part[None], (count,) + part.shape).reshape(-1, lanes)
        part = lax.all_to_all(spread, stage, 0, 0, tiled=True)
    flat = part.astype(jnp.float32).reshape(-1)
    out, start = [], 0
    for g, n in zip(grads, sizes):
        out.append(flat[start : start + n].reshape(g.shape))
        start += n
    return out


def solution(mesh):
    space, group = mesh.shape["space"], mesh.shape["group"]
    sub = Mesh(
        mesh.devices.reshape(space // 8, 4, 2, group // 2, 2),
        ("zl", "x", "c", "y", "zh"),
    )
    S, G = SPACE, GROUP
    in_specs = (
        P(G, S, None),
        P(G, None, S),
        P(G, None),
        P(G, S),
        P(G, S, None),
        P(G, S, None),
        P(G, S, None),
        P(G, None, S),
        P(),
        P(),
        P(),
        P(),
        P(),
    )
    out_specs = (P(G, None, S), P(), P(), P(), P(), P())
    return jax.shard_map(
        per_device, mesh=sub, in_specs=in_specs, out_specs=out_specs, check_vma=False
    )
```

```python
import jax
import jax.numpy as jnp
from jax import lax
from jax.sharding import Mesh, PartitionSpec as P

RANGE_TOP = 48.0


def padded(cells, sides, width):
    for axis, dim in sides:
        count = lax.axis_size(axis)
        head = lax.slice_in_dim(cells, 0, width, axis=dim)
        tail = lax.slice_in_dim(cells, cells.shape[dim] - width, cells.shape[dim], axis=dim)
        cells = jnp.concatenate(
            [
                lax.ppermute(tail, axis, [(i, (i + 1) % count) for i in range(count)]),
                cells,
                lax.ppermute(head, axis, [((i + 1) % count, i) for i in range(count)]),
            ],
            axis=dim,
        )
    return cells


def tiled(block, count):
    return jnp.concatenate([block] * count, axis=1)


def energy(params, table_feats, table_pos, neighbours, edge_mask, shift_ids, cell_box):
    w_zero, w_real, w_imag, radial, readout = params
    target_count, degree = neighbours.shape
    levels, channels = radial.shape
    flat_ids = neighbours.T.reshape(-1)
    shift_list = shift_ids.T.reshape(-1)
    live = edge_mask.T.reshape(-1)
    offset = (
        jnp.stack([shift_list // 9 - 1, shift_list // 3 % 3 - 1, shift_list % 3 - 1]).astype(
            jnp.float32
        )
        * cell_box[:, None]
    )
    edge_vec = (
        jnp.take(table_pos, flat_ids, axis=1)
        + offset
        - tiled(table_pos[:, :target_count], degree)
    )
    delta_one, delta_two, delta_three = (edge_vec[0], edge_vec[1], edge_vec[2])
    planar = jnp.sqrt(delta_one * delta_one + delta_two * delta_two + 1.0)
    radius = jnp.sqrt(planar * planar + delta_three * delta_three)
    cos_phi = (delta_one / planar)[:, None]
    sin_phi = (delta_two / planar)[:, None]
    cos_tilt = (delta_three / radius)[:, None]
    sin_tilt = (planar / radius)[:, None]
    spacing = RANGE_TOP / (levels - 1)
    centers = jnp.arange(levels, dtype=jnp.float32) * spacing
    basis_vals = jnp.exp(-jnp.square((radius[:, None] - centers[None, :]) / (2.0 * spacing)))
    radial_gain = jnp.dot(basis_vals, radial, precision=lax.Precision.HIGHEST)
    c = channels
    source = jnp.take(table_feats, flat_ids, axis=0).astype(jnp.float32)
    zero_part = source[:, 0 : 7 * c]
    plus_part = source[:, 7 * c : 13 * c]
    minus_part = source[:, 13 * c : 19 * c]
    plus_turn = cos_phi * plus_part + sin_phi * minus_part
    minus_turn = cos_phi * minus_part - sin_phi * plus_part
    upper = zero_part[:, c:]
    upper_tilt = cos_tilt * upper - sin_tilt * plus_turn
    plus_tilt = sin_tilt * upper + cos_tilt * plus_turn
    gain_six = tiled(radial_gain, 6)
    in_zero = (
        jnp.concatenate([zero_part[:, :c], upper_tilt], 1) * tiled(radial_gain, 7)
    ).astype(jnp.bfloat16)
    in_plus = (plus_tilt * gain_six).astype(jnp.bfloat16)
    in_minus = (minus_turn * gain_six).astype(jnp.bfloat16)
    weight_zero = w_zero.astype(jnp.bfloat16)
    weight_real = w_real.astype(jnp.bfloat16)
    weight_imag = w_imag.astype(jnp.bfloat16)
    out_zero = jnp.dot(in_zero, weight_zero, preferred_element_type=jnp.float32)
    out_plus = jnp.dot(in_plus, weight_real, preferred_element_type=jnp.float32) - jnp.dot(
        in_minus, weight_imag, preferred_element_type=jnp.float32
    )
    out_minus = jnp.dot(in_plus, weight_imag, preferred_element_type=jnp.float32) + jnp.dot(
        in_minus, weight_real, preferred_element_type=jnp.float32
    )
    zero_upper = out_zero[:, c:]
    upper_back = cos_tilt * zero_upper + sin_tilt * out_plus
    plus_back = cos_tilt * out_plus - sin_tilt * zero_upper
    plus_final = cos_phi * plus_back - sin_phi * out_minus
    minus_final = cos_phi * out_minus + sin_phi * plus_back
    message = jnp.concatenate([out_zero[:, :c], upper_back, plus_final, minus_final], 1)
    message = message * live.astype(jnp.float32)[:, None]
    summed = message[:target_count]
    for k in range(1, degree):
        summed = summed + message[k * target_count : (k + 1) * target_count]
    summed = summed / degree
    updated = table_feats[:target_count].astype(jnp.float32) + summed
    square = updated * updated
    total = square[:, :c]
    for k in range(1, 19):
        total = total + square[:, k * c : (k + 1) * c]
    invariant = updated[:, :c] + total / 19
    return jnp.sum(jax.nn.silu(invariant) * readout[None, :])


def per_device(
    features,
    positions,
    cell_box,
    send_rows,
    neighbours,
    edge_mask,
    shift_ids,
    target_forces,
    w_zero,
    w_real,
    w_imag,
    radial,
    readout,
):
    atom_feats = features[0]
    atom_pos = positions[0]
    box_sides = cell_box[0]
    sends = send_rows[0]
    neighbour_ids = neighbours[0]
    edge_live = edge_mask[0]
    shift_list = shift_ids[0]
    wanted = target_forces[0]
    own_count = atom_feats.shape[0]
    ghosts = sends.shape[0] // 2
    part_count = lax.axis_size(SPACE)
    listed = jnp.take(atom_feats, sends, axis=0)
    beside_all = padded(listed, ((SPACE, 0),), ghosts)
    table_feats = jnp.concatenate([atom_feats, beside_all[:ghosts], beside_all[3 * ghosts :]], 0)
    spots = jnp.take(atom_pos, sends, axis=1)
    nearby = padded(spots, ((SPACE, 1),), ghosts)
    table_pos = jnp.concatenate([atom_pos, nearby[:, :ghosts], nearby[:, 3 * ghosts :]], 1)
    params = (
        w_zero.astype(jnp.float32),
        w_real.astype(jnp.float32),
        w_imag.astype(jnp.float32),
        radial,
        readout,
    )

    def position_grad(weights):
        return jax.grad(energy, 2)(
            weights, table_feats, table_pos, neighbour_ids, edge_live, shift_list, box_sides
        )

    grad_pos, pullback = jax.vjp(position_grad, params)
    ghost_grad = grad_pos[:, own_count:]
    backed = padded(ghost_grad, ((SPACE, 1),), ghosts)
    returned = jnp.concatenate([backed[:, :ghosts], backed[:, 3 * ghosts :]], 1)
    onehot = (sends[:, None] == jnp.arange(own_count, dtype=jnp.int32)[None, :]).astype(jnp.float32)
    added = jnp.dot(returned, onehot, precision=lax.Precision.HIGHEST)
    forces = -(grad_pos[:, :own_count] + added)
    loss_weights = 2.0 * (forces - wanted) / (part_count * own_count)
    picked = jnp.take(loss_weights, sends, axis=1)
    shared = padded(picked, ((SPACE, 1),), ghosts)
    table_u = jnp.concatenate([loss_weights, shared[:, :ghosts], shared[:, 3 * ghosts :]], 1)
    (grads,) = pullback(-table_u)
    grad_zero, grad_real, grad_imag, grad_radial, grad_readout = all_sum(grads)
    return (forces[None], grad_zero, grad_real, grad_imag, grad_radial, grad_readout)


SPACE = ("zl", "x", "c")
GROUP = ("y", "zh")
STAGES = (("c",), ("x", "y"), ("zh", "zl"))


def all_sum(grads):
    lanes = 128
    sizes = [g.size for g in grads]
    total = sum(sizes)
    devices = 1
    for stage in STAGES:
        devices *= lax.axis_size(stage)
    rows = -(-total // lanes)
    rows = -(-rows // (devices * 16)) * devices * 16
    flat = jnp.concatenate(
        [g.reshape(-1) for g in grads] + [jnp.zeros((rows * lanes - total,), jnp.float32)]
    )
    part = flat.astype(jnp.bfloat16).reshape(rows, lanes)
    for stage in STAGES:
        count = lax.axis_size(stage)
        got = lax.all_to_all(part, stage, 0, 0, tiled=True)
        part = got.reshape(count, -1, lanes).astype(jnp.float32).sum(0).astype(jnp.bfloat16)
    for stage in STAGES[::-1]:
        count = lax.axis_size(stage)
        spread = jnp.broadcast_to(part[None], (count,) + part.shape).reshape(-1, lanes)
        part = lax.all_to_all(spread, stage, 0, 0, tiled=True)
    flat = part.astype(jnp.float32).reshape(-1)
    out, start = [], 0
    for g, n in zip(grads, sizes):
        out.append(flat[start : start + n].reshape(g.shape))
        start += n
    return out


def solution(mesh):
    space, group = mesh.shape["space"], mesh.shape["group"]
    sub = Mesh(
        mesh.devices.reshape(space // 8, 4, 2, group // 2, 2),
        ("zl", "x", "c", "y", "zh"),
    )
    S, G = SPACE, GROUP
    in_specs = (
        P(G, S, None),
        P(G, None, S),
        P(G, None),
        P(G, S),
        P(G, S, None),
        P(G, S, None),
        P(G, S, None),
        P(G, None, S),
        P(),
        P(),
        P(),
        P(),
        P(),
    )
    out_specs = (P(G, None, S), P(), P(), P(), P(), P())
    return jax.shard_map(
        per_device, mesh=sub, in_specs=in_specs, out_specs=out_specs, check_vma=False
    )
```

```python
import jax
import jax.numpy as jnp
from jax import lax
from jax.sharding import Mesh, PartitionSpec as P

RANGE_TOP = 48.0


def exchange(cells, dim, width):
    count = lax.axis_size(SPACE)
    head = lax.slice_in_dim(cells, 0, width, axis=dim)
    tail = lax.slice_in_dim(cells, cells.shape[dim] - width, cells.shape[dim], axis=dim)
    from_below = lax.ppermute(tail, SPACE, [(i, (i + 1) % count) for i in range(count)])
    from_above = lax.ppermute(head, SPACE, [((i + 1) % count, i) for i in range(count)])
    return from_below, from_above


def tiled(block, count):
    return jnp.concatenate([block] * count, axis=1)


def energy(params, table_feats, table_pos, neighbours, edge_mask, shift_ids, cell_box):
    w_zero, w_real, w_imag, radial, readout = params
    target_count, degree = neighbours.shape
    levels, channels = radial.shape
    flat_ids = neighbours.T.reshape(-1)
    shift_list = shift_ids.T.reshape(-1)
    live = edge_mask.T.reshape(-1)
    offset = (
        jnp.stack([shift_list // 9 - 1, shift_list // 3 % 3 - 1, shift_list % 3 - 1]).astype(
            jnp.float32
        )
        * cell_box[:, None]
    )
    edge_vec = (
        jnp.take(table_pos, flat_ids, axis=1)
        + offset
        - tiled(table_pos[:, :target_count], degree)
    )
    delta_one, delta_two, delta_three = (edge_vec[0], edge_vec[1], edge_vec[2])
    planar = jnp.sqrt(delta_one * delta_one + delta_two * delta_two + 1.0)
    radius = jnp.sqrt(planar * planar + delta_three * delta_three)
    cos_phi = (delta_one / planar)[:, None]
    sin_phi = (delta_two / planar)[:, None]
    cos_tilt = (delta_three / radius)[:, None]
    sin_tilt = (planar / radius)[:, None]
    spacing = RANGE_TOP / (levels - 1)
    centers = jnp.arange(levels, dtype=jnp.float32) * spacing
    basis_vals = jnp.exp(-jnp.square((radius[:, None] - centers[None, :]) / (2.0 * spacing)))
    radial_gain = jnp.dot(basis_vals, radial, precision=lax.Precision.HIGHEST)
    c = channels
    source = jnp.take(table_feats, flat_ids, axis=0).astype(jnp.float32)
    zero_part = source[:, 0 : 7 * c]
    plus_part = source[:, 7 * c : 13 * c]
    minus_part = source[:, 13 * c : 19 * c]
    plus_turn = cos_phi * plus_part + sin_phi * minus_part
    minus_turn = cos_phi * minus_part - sin_phi * plus_part
    upper = zero_part[:, c:]
    upper_tilt = cos_tilt * upper - sin_tilt * plus_turn
    plus_tilt = sin_tilt * upper + cos_tilt * plus_turn
    gain_six = tiled(radial_gain, 6)
    in_zero = (
        jnp.concatenate([zero_part[:, :c], upper_tilt], 1) * tiled(radial_gain, 7)
    ).astype(jnp.bfloat16)
    in_plus = (plus_tilt * gain_six).astype(jnp.bfloat16)
    in_minus = (minus_turn * gain_six).astype(jnp.bfloat16)
    weight_zero = w_zero.astype(jnp.bfloat16)
    weight_real = w_real.astype(jnp.bfloat16)
    weight_imag = w_imag.astype(jnp.bfloat16)
    out_zero = jnp.dot(in_zero, weight_zero, preferred_element_type=jnp.float32)
    out_plus = jnp.dot(in_plus, weight_real, preferred_element_type=jnp.float32) - jnp.dot(
        in_minus, weight_imag, preferred_element_type=jnp.float32
    )
    out_minus = jnp.dot(in_plus, weight_imag, preferred_element_type=jnp.float32) + jnp.dot(
        in_minus, weight_real, preferred_element_type=jnp.float32
    )
    zero_upper = out_zero[:, c:]
    upper_back = cos_tilt * zero_upper + sin_tilt * out_plus
    plus_back = cos_tilt * out_plus - sin_tilt * zero_upper
    plus_final = cos_phi * plus_back - sin_phi * out_minus
    minus_final = cos_phi * out_minus + sin_phi * plus_back
    message = jnp.concatenate([out_zero[:, :c], upper_back, plus_final, minus_final], 1)
    message = message * live.astype(jnp.float32)[:, None]
    summed = message[:target_count]
    for k in range(1, degree):
        summed = summed + message[k * target_count : (k + 1) * target_count]
    summed = summed / degree
    updated = table_feats[:target_count].astype(jnp.float32) + summed
    square = updated * updated
    total = square[:, :c]
    for k in range(1, 19):
        total = total + square[:, k * c : (k + 1) * c]
    invariant = updated[:, :c] + total / 19
    return jnp.sum(jax.nn.silu(invariant) * readout[None, :])


def per_device(
    features,
    positions,
    cell_box,
    send_rows,
    neighbours,
    edge_mask,
    shift_ids,
    target_forces,
    w_zero,
    w_real,
    w_imag,
    radial,
    readout,
):
    atom_feats = features[0]
    atom_pos = positions[0]
    box_sides = cell_box[0]
    sends = send_rows[0]
    neighbour_ids = neighbours[0]
    edge_live = edge_mask[0]
    shift_list = shift_ids[0]
    wanted = target_forces[0]
    own_count = atom_feats.shape[0]
    ghosts = sends.shape[0] // 2
    part_count = lax.axis_size(SPACE)
    width = atom_feats.shape[1]
    listed = jnp.take(atom_feats, sends, axis=0).astype(jnp.float32)
    spots = jnp.take(atom_pos, sends, axis=1)
    lanes = -(-(width + 3) // 128) * 128
    both = jnp.concatenate(
        [listed, spots.T, jnp.zeros((listed.shape[0], lanes - width - 3), jnp.float32)], 1
    )
    below, above = exchange(both, 0, ghosts)
    table_feats = jnp.concatenate(
        [atom_feats, below[:, :width].astype(atom_feats.dtype), above[:, :width].astype(atom_feats.dtype)], 0
    )
    table_pos = jnp.concatenate(
        [atom_pos, below[:, width : width + 3].T, above[:, width : width + 3].T], 1
    )
    params = (
        w_zero.astype(jnp.float32),
        w_real.astype(jnp.float32),
        w_imag.astype(jnp.float32),
        radial,
        readout,
    )

    def position_grad(weights):
        return jax.grad(energy, 2)(
            weights, table_feats, table_pos, neighbour_ids, edge_live, shift_list, box_sides
        )

    grad_pos, pullback = jax.vjp(position_grad, params)
    ghost_grad = grad_pos[:, own_count:]
    returned = jnp.concatenate(exchange(ghost_grad, 1, ghosts), 1)
    onehot = (sends[:, None] == jnp.arange(own_count, dtype=jnp.int32)[None, :]).astype(jnp.float32)
    added = jnp.dot(returned, onehot, precision=lax.Precision.HIGHEST)
    forces = -(grad_pos[:, :own_count] + added)
    loss_weights = 2.0 * (forces - wanted) / (part_count * own_count)
    picked = jnp.take(loss_weights, sends, axis=1)
    table_u = jnp.concatenate([loss_weights, *exchange(picked, 1, ghosts)], 1)
    (grads,) = pullback(-table_u)
    grad_zero, grad_real, grad_imag, grad_radial, grad_readout = all_sum(grads)
    return (forces[None], grad_zero, grad_real, grad_imag, grad_radial, grad_readout)


SPACE = ("zl", "x", "c")
GROUP = ("y", "zh")
STAGES = (("c",), ("x", "y"), ("zh", "zl"))


def all_sum(grads):
    lanes = 128
    blocks = []
    for g in grads:
        g = g.reshape(-1, g.shape[-1]) if g.ndim > 1 else g.reshape(1, -1)
        g = jnp.pad(g, ((0, -g.shape[0] % 16), (0, 0)))
        blocks += [g[:, j : j + lanes] for j in range(0, g.shape[1], lanes)]
    total = sum(b.shape[0] for b in blocks)
    devices = 1
    for stage in STAGES:
        devices *= lax.axis_size(stage)
    rows = -(-total // (devices * 16)) * devices * 16
    blocks.append(jnp.zeros((rows - total, lanes), jnp.float32))
    part = jnp.concatenate(blocks, 0).astype(jnp.bfloat16)
    for stage in STAGES:
        count = lax.axis_size(stage)
        got = lax.all_to_all(part, stage, 0, 0, tiled=True)
        part = got.reshape(count, -1, lanes).astype(jnp.float32).sum(0).astype(jnp.bfloat16)
    for stage in STAGES[::-1]:
        count = lax.axis_size(stage)
        spread = jnp.broadcast_to(part[None], (count,) + part.shape).reshape(-1, lanes)
        part = lax.all_to_all(spread, stage, 0, 0, tiled=True)
    out, start = [], 0
    for g in grads:
        height = g.shape[0] if g.ndim > 1 else 1
        pieces = []
        for _ in range(0, g.shape[-1], lanes):
            pieces.append(part[start : start + height])
            start += height + (-height % 16)
        out.append(jnp.concatenate(pieces, 1).astype(jnp.float32).reshape(g.shape))
    return out


def solution(mesh):
    space, group = mesh.shape["space"], mesh.shape["group"]
    sub = Mesh(
        mesh.devices.reshape(space // 8, 4, 2, group // 2, 2),
        ("zl", "x", "c", "y", "zh"),
    )
    S, G = SPACE, GROUP
    in_specs = (
        P(G, S, None),
        P(G, None, S),
        P(G, None),
        P(G, S),
        P(G, S, None),
        P(G, S, None),
        P(G, S, None),
        P(G, None, S),
        P(),
        P(),
        P(),
        P(),
        P(),
    )
    out_specs = (P(G, None, S), P(), P(), P(), P(), P())
    return jax.shard_map(
        per_device, mesh=sub, in_specs=in_specs, out_specs=out_specs, check_vma=False
    )
```

```python
import jax
import jax.numpy as jnp
from jax import lax
from jax.sharding import Mesh, PartitionSpec as P

RANGE_TOP = 48.0


def exchange(cells, dim, width):
    count = lax.axis_size(SPACE)
    head = lax.slice_in_dim(cells, 0, width, axis=dim)
    tail = lax.slice_in_dim(cells, cells.shape[dim] - width, cells.shape[dim], axis=dim)
    from_below = lax.ppermute(tail, SPACE, [(i, (i + 1) % count) for i in range(count)])
    from_above = lax.ppermute(head, SPACE, [((i + 1) % count, i) for i in range(count)])
    return from_below, from_above


def blocks_matrix(count, width):
    rows = lax.broadcasted_iota(jnp.int32, (count * width, width), 0)
    cols = lax.broadcasted_iota(jnp.int32, (count * width, width), 1)
    return (rows % width == cols).astype(jnp.float32)


def tiled(block, count):
    return jnp.dot(block, blocks_matrix(count, block.shape[1]).T, precision=lax.Precision.HIGHEST)


def block_sum(wide, width):
    return jnp.dot(wide, blocks_matrix(wide.shape[1] // width, width), precision=lax.Precision.HIGHEST)


def energy(params, table_feats, table_pos, neighbours, edge_mask, shift_ids, cell_box):
    w_zero, w_real, w_imag, radial, readout = params
    target_count, degree = neighbours.shape
    levels, channels = radial.shape
    flat_ids = neighbours.T.reshape(-1)
    shift_list = shift_ids.T.reshape(-1)
    live = edge_mask.T.reshape(-1)
    offset = (
        jnp.stack([shift_list // 9 - 1, shift_list // 3 % 3 - 1, shift_list % 3 - 1]).astype(
            jnp.float32
        )
        * cell_box[:, None]
    )
    edge_vec = (
        jnp.take(table_pos, flat_ids, axis=1)
        + offset
        - jnp.concatenate([table_pos[:, :target_count]] * degree, axis=1)
    )
    delta_one, delta_two, delta_three = (edge_vec[0], edge_vec[1], edge_vec[2])
    planar = jnp.sqrt(delta_one * delta_one + delta_two * delta_two + 1.0)
    radius = jnp.sqrt(planar * planar + delta_three * delta_three)
    cos_phi = (delta_one / planar)[:, None]
    sin_phi = (delta_two / planar)[:, None]
    cos_tilt = (delta_three / radius)[:, None]
    sin_tilt = (planar / radius)[:, None]
    spacing = RANGE_TOP / (levels - 1)
    centers = jnp.arange(levels, dtype=jnp.float32) * spacing
    basis_vals = jnp.exp(-jnp.square((radius[:, None] - centers[None, :]) / (2.0 * spacing)))
    radial_gain = jnp.dot(basis_vals, radial, precision=lax.Precision.HIGHEST)
    c = channels
    source = jnp.take(table_feats, flat_ids, axis=0).astype(jnp.float32)
    zero_part = source[:, 0 : 7 * c]
    plus_part = source[:, 7 * c : 13 * c]
    minus_part = source[:, 13 * c : 19 * c]
    plus_turn = cos_phi * plus_part + sin_phi * minus_part
    minus_turn = cos_phi * minus_part - sin_phi * plus_part
    upper = zero_part[:, c:]
    upper_tilt = cos_tilt * upper - sin_tilt * plus_turn
    plus_tilt = sin_tilt * upper + cos_tilt * plus_turn
    gain_six = tiled(radial_gain, 6)
    in_zero = (
        jnp.concatenate([zero_part[:, :c], upper_tilt], 1) * tiled(radial_gain, 7)
    ).astype(jnp.bfloat16)
    in_plus = (plus_tilt * gain_six).astype(jnp.bfloat16)
    in_minus = (minus_turn * gain_six).astype(jnp.bfloat16)
    weight_zero = w_zero.astype(jnp.bfloat16)
    weight_real = w_real.astype(jnp.bfloat16)
    weight_imag = w_imag.astype(jnp.bfloat16)
    out_zero = jnp.dot(in_zero, weight_zero, preferred_element_type=jnp.float32)
    out_plus = jnp.dot(in_plus, weight_real, preferred_element_type=jnp.float32) - jnp.dot(
        in_minus, weight_imag, preferred_element_type=jnp.float32
    )
    out_minus = jnp.dot(in_plus, weight_imag, preferred_element_type=jnp.float32) + jnp.dot(
        in_minus, weight_real, preferred_element_type=jnp.float32
    )
    zero_upper = out_zero[:, c:]
    upper_back = cos_tilt * zero_upper + sin_tilt * out_plus
    plus_back = cos_tilt * out_plus - sin_tilt * zero_upper
    plus_final = cos_phi * plus_back - sin_phi * out_minus
    minus_final = cos_phi * out_minus + sin_phi * plus_back
    message = jnp.concatenate([out_zero[:, :c], upper_back, plus_final, minus_final], 1)
    message = message * live.astype(jnp.float32)[:, None]
    summed = message[:target_count]
    for k in range(1, degree):
        summed = summed + message[k * target_count : (k + 1) * target_count]
    summed = summed / degree
    updated = table_feats[:target_count].astype(jnp.float32) + summed
    square = updated * updated
    total = block_sum(square, c)
    invariant = updated[:, :c] + total / 19
    return jnp.sum(jax.nn.silu(invariant) * readout[None, :])


def per_device(
    features,
    positions,
    cell_box,
    send_rows,
    neighbours,
    edge_mask,
    shift_ids,
    target_forces,
    w_zero,
    w_real,
    w_imag,
    radial,
    readout,
):
    atom_feats = features[0]
    atom_pos = positions[0]
    box_sides = cell_box[0]
    sends = send_rows[0]
    neighbour_ids = neighbours[0]
    edge_live = edge_mask[0]
    shift_list = shift_ids[0]
    wanted = target_forces[0]
    own_count = atom_feats.shape[0]
    ghosts = sends.shape[0] // 2
    part_count = lax.axis_size(SPACE)
    width = atom_feats.shape[1]
    listed = jnp.take(atom_feats, sends, axis=0).astype(jnp.float32)
    spots = jnp.take(atom_pos, sends, axis=1)
    lanes = -(-(width + 3) // 128) * 128
    both = jnp.concatenate(
        [listed, spots.T, jnp.zeros((listed.shape[0], lanes - width - 3), jnp.float32)], 1
    )
    below, above = exchange(both, 0, ghosts)
    table_feats = jnp.concatenate(
        [atom_feats, below[:, :width].astype(atom_feats.dtype), above[:, :width].astype(atom_feats.dtype)], 0
    )
    table_pos = jnp.concatenate(
        [atom_pos, below[:, width : width + 3].T, above[:, width : width + 3].T], 1
    )
    params = (
        w_zero.astype(jnp.float32),
        w_real.astype(jnp.float32),
        w_imag.astype(jnp.float32),
        radial,
        readout,
    )

    def position_grad(weights):
        return jax.grad(energy, 2)(
            weights, table_feats, table_pos, neighbour_ids, edge_live, shift_list, box_sides
        )

    grad_pos, pullback = jax.vjp(position_grad, params)
    ghost_grad = grad_pos[:, own_count:]
    returned = jnp.concatenate(exchange(ghost_grad, 1, ghosts), 1)
    onehot = (sends[:, None] == jnp.arange(own_count, dtype=jnp.int32)[None, :]).astype(jnp.float32)
    added = jnp.dot(returned, onehot, precision=lax.Precision.HIGHEST)
    forces = -(grad_pos[:, :own_count] + added)
    loss_weights = 2.0 * (forces - wanted) / (part_count * own_count)
    picked = jnp.take(loss_weights, sends, axis=1)
    table_u = jnp.concatenate([loss_weights, *exchange(picked, 1, ghosts)], 1)
    (grads,) = pullback(-table_u)
    grad_zero, grad_real, grad_imag, grad_radial, grad_readout = all_sum(grads)
    return (forces[None], grad_zero, grad_real, grad_imag, grad_radial, grad_readout)


SPACE = ("zl", "x", "c")
GROUP = ("y", "zh")
STAGES = (("c",), ("x", "y"), ("zh", "zl"))


def all_sum(grads):
    lanes = 128
    blocks = []
    for g in grads:
        g = g.reshape(-1, g.shape[-1]) if g.ndim > 1 else g.reshape(1, -1)
        g = jnp.pad(g, ((0, -g.shape[0] % 16), (0, 0)))
        blocks += [g[:, j : j + lanes] for j in range(0, g.shape[1], lanes)]
    total = sum(b.shape[0] for b in blocks)
    devices = 1
    for stage in STAGES:
        devices *= lax.axis_size(stage)
    rows = -(-total // (devices * 16)) * devices * 16
    blocks.append(jnp.zeros((rows - total, lanes), jnp.float32))
    part = jnp.concatenate(blocks, 0).astype(jnp.bfloat16)
    for stage in STAGES:
        count = lax.axis_size(stage)
        got = lax.all_to_all(part, stage, 0, 0, tiled=True)
        part = got.reshape(count, -1, lanes).astype(jnp.float32).sum(0).astype(jnp.bfloat16)
    for stage in STAGES[::-1]:
        count = lax.axis_size(stage)
        spread = jnp.broadcast_to(part[None], (count,) + part.shape).reshape(-1, lanes)
        part = lax.all_to_all(spread, stage, 0, 0, tiled=True)
    out, start = [], 0
    for g in grads:
        height = g.shape[0] if g.ndim > 1 else 1
        pieces = []
        for _ in range(0, g.shape[-1], lanes):
            pieces.append(part[start : start + height])
            start += height + (-height % 16)
        out.append(jnp.concatenate(pieces, 1).astype(jnp.float32).reshape(g.shape))
    return out


def solution(mesh):
    space, group = mesh.shape["space"], mesh.shape["group"]
    sub = Mesh(
        mesh.devices.reshape(space // 8, 4, 2, group // 2, 2),
        ("zl", "x", "c", "y", "zh"),
    )
    S, G = SPACE, GROUP
    in_specs = (
        P(G, S, None),
        P(G, None, S),
        P(G, None),
        P(G, S),
        P(G, S, None),
        P(G, S, None),
        P(G, S, None),
        P(G, None, S),
        P(),
        P(),
        P(),
        P(),
        P(),
    )
    out_specs = (P(G, None, S), P(), P(), P(), P(), P())
    return jax.shard_map(
        per_device, mesh=sub, in_specs=in_specs, out_specs=out_specs, check_vma=False
    )
```

```python
import functools

import jax
import jax.numpy as jnp
from jax import lax
from jax.sharding import Mesh, PartitionSpec as P

RANGE_TOP = 48.0


def exchange(cells, dim, width):
    count = lax.axis_size(SPACE)
    head = lax.slice_in_dim(cells, 0, width, axis=dim)
    tail = lax.slice_in_dim(cells, cells.shape[dim] - width, cells.shape[dim], axis=dim)
    from_below = lax.ppermute(tail, SPACE, [(i, (i + 1) % count) for i in range(count)])
    from_above = lax.ppermute(head, SPACE, [((i + 1) % count, i) for i in range(count)])
    return from_below, from_above


@functools.partial(jax.custom_vjp, nondiff_argnums=(1,))
def tiled(block, count):
    return jnp.concatenate([block] * count, axis=1)


def tiled_fwd(block, count):
    return tiled(block, count), None


def tiled_bwd(count, unused, grad):
    return (block_sum(grad, count),)


@functools.partial(jax.custom_vjp, nondiff_argnums=(1,))
def block_sum(wide, count):
    width = wide.shape[1] // count
    total = wide[:, :width]
    for k in range(1, count):
        total = total + wide[:, k * width : (k + 1) * width]
    return total


def block_sum_fwd(wide, count):
    return block_sum(wide, count), None


def block_sum_bwd(count, unused, grad):
    return (tiled(grad, count),)


tiled.defvjp(tiled_fwd, tiled_bwd)
block_sum.defvjp(block_sum_fwd, block_sum_bwd)


def energy(params, table_feats, table_pos, neighbours, edge_mask, shift_ids, cell_box):
    w_zero, w_real, w_imag, radial, readout = params
    target_count, degree = neighbours.shape
    levels, channels = radial.shape
    flat_ids = neighbours.T.reshape(-1)
    shift_list = shift_ids.T.reshape(-1)
    live = edge_mask.T.reshape(-1)
    offset = (
        jnp.stack([shift_list // 9 - 1, shift_list // 3 % 3 - 1, shift_list % 3 - 1]).astype(
            jnp.float32
        )
        * cell_box[:, None]
    )
    edge_vec = (
        jnp.take(table_pos, flat_ids, axis=1)
        + offset
        - jnp.concatenate([table_pos[:, :target_count]] * degree, axis=1)
    )
    delta_one, delta_two, delta_three = (edge_vec[0], edge_vec[1], edge_vec[2])
    planar = jnp.sqrt(delta_one * delta_one + delta_two * delta_two + 1.0)
    radius = jnp.sqrt(planar * planar + delta_three * delta_three)
    cos_phi = (delta_one / planar)[:, None]
    sin_phi = (delta_two / planar)[:, None]
    cos_tilt = (delta_three / radius)[:, None]
    sin_tilt = (planar / radius)[:, None]
    spacing = RANGE_TOP / (levels - 1)
    centers = jnp.arange(levels, dtype=jnp.float32) * spacing
    basis_vals = jnp.exp(-jnp.square((radius[:, None] - centers[None, :]) / (2.0 * spacing)))
    radial_gain = jnp.dot(basis_vals, radial, precision=lax.Precision.HIGHEST)
    c = channels
    source = jnp.take(table_feats, flat_ids, axis=0).astype(jnp.float32)
    zero_part = source[:, 0 : 7 * c]
    plus_part = source[:, 7 * c : 13 * c]
    minus_part = source[:, 13 * c : 19 * c]
    plus_turn = cos_phi * plus_part + sin_phi * minus_part
    minus_turn = cos_phi * minus_part - sin_phi * plus_part
    upper = zero_part[:, c:]
    upper_tilt = cos_tilt * upper - sin_tilt * plus_turn
    plus_tilt = sin_tilt * upper + cos_tilt * plus_turn
    gain_six = tiled(radial_gain, 6)
    in_zero = (
        jnp.concatenate([zero_part[:, :c], upper_tilt], 1) * tiled(radial_gain, 7)
    ).astype(jnp.bfloat16)
    in_plus = (plus_tilt * gain_six).astype(jnp.bfloat16)
    in_minus = (minus_turn * gain_six).astype(jnp.bfloat16)
    weight_zero = w_zero.astype(jnp.bfloat16)
    weight_real = w_real.astype(jnp.bfloat16)
    weight_imag = w_imag.astype(jnp.bfloat16)
    out_zero = jnp.dot(in_zero, weight_zero, preferred_element_type=jnp.float32)
    out_plus = jnp.dot(in_plus, weight_real, preferred_element_type=jnp.float32) - jnp.dot(
        in_minus, weight_imag, preferred_element_type=jnp.float32
    )
    out_minus = jnp.dot(in_plus, weight_imag, preferred_element_type=jnp.float32) + jnp.dot(
        in_minus, weight_real, preferred_element_type=jnp.float32
    )
    zero_upper = out_zero[:, c:]
    upper_back = cos_tilt * zero_upper + sin_tilt * out_plus
    plus_back = cos_tilt * out_plus - sin_tilt * zero_upper
    plus_final = cos_phi * plus_back - sin_phi * out_minus
    minus_final = cos_phi * out_minus + sin_phi * plus_back
    message = jnp.concatenate([out_zero[:, :c], upper_back, plus_final, minus_final], 1)
    message = message * live.astype(jnp.float32)[:, None]
    summed = message[:target_count]
    for k in range(1, degree):
        summed = summed + message[k * target_count : (k + 1) * target_count]
    summed = summed / degree
    updated = table_feats[:target_count].astype(jnp.float32) + summed
    square = updated * updated
    total = block_sum(square, square.shape[1] // c)
    invariant = updated[:, :c] + total / 19
    return jnp.sum(jax.nn.silu(invariant) * readout[None, :])


def per_device(
    features,
    positions,
    cell_box,
    send_rows,
    neighbours,
    edge_mask,
    shift_ids,
    target_forces,
    w_zero,
    w_real,
    w_imag,
    radial,
    readout,
):
    atom_feats = features[0]
    atom_pos = positions[0]
    box_sides = cell_box[0]
    sends = send_rows[0]
    neighbour_ids = neighbours[0]
    edge_live = edge_mask[0]
    shift_list = shift_ids[0]
    wanted = target_forces[0]
    own_count = atom_feats.shape[0]
    ghosts = sends.shape[0] // 2
    part_count = lax.axis_size(SPACE)
    width = atom_feats.shape[1]
    listed = jnp.take(atom_feats, sends, axis=0).astype(jnp.float32)
    spots = jnp.take(atom_pos, sends, axis=1)
    lanes = -(-(width + 3) // 128) * 128
    both = jnp.concatenate(
        [listed, spots.T, jnp.zeros((listed.shape[0], lanes - width - 3), jnp.float32)], 1
    )
    below, above = exchange(both, 0, ghosts)
    table_feats = jnp.concatenate(
        [atom_feats, below[:, :width].astype(atom_feats.dtype), above[:, :width].astype(atom_feats.dtype)], 0
    )
    table_pos = jnp.concatenate(
        [atom_pos, below[:, width : width + 3].T, above[:, width : width + 3].T], 1
    )
    params = (
        w_zero.astype(jnp.float32),
        w_real.astype(jnp.float32),
        w_imag.astype(jnp.float32),
        radial,
        readout,
    )

    def position_grad(weights):
        return jax.grad(energy, 2)(
            weights, table_feats, table_pos, neighbour_ids, edge_live, shift_list, box_sides
        )

    grad_pos, pullback = jax.vjp(position_grad, params)
    ghost_grad = grad_pos[:, own_count:]
    returned = jnp.concatenate(exchange(ghost_grad, 1, ghosts), 1)
    onehot = (sends[:, None] == jnp.arange(own_count, dtype=jnp.int32)[None, :]).astype(jnp.float32)
    added = jnp.dot(returned, onehot, precision=lax.Precision.HIGHEST)
    forces = -(grad_pos[:, :own_count] + added)
    loss_weights = 2.0 * (forces - wanted) / (part_count * own_count)
    picked = jnp.take(loss_weights, sends, axis=1)
    table_u = jnp.concatenate([loss_weights, *exchange(picked, 1, ghosts)], 1)
    (grads,) = pullback(-table_u)
    grad_zero, grad_real, grad_imag, grad_radial, grad_readout = all_sum(grads)
    return (forces[None], grad_zero, grad_real, grad_imag, grad_radial, grad_readout)


SPACE = ("zl", "x", "c")
GROUP = ("y", "zh")
STAGES = (("c",), ("x", "y"), ("zh", "zl"))


def all_sum(grads):
    lanes = 128
    blocks = []
    for g in grads:
        g = g.reshape(-1, g.shape[-1]) if g.ndim > 1 else g.reshape(1, -1)
        g = jnp.pad(g, ((0, -g.shape[0] % 16), (0, 0)))
        blocks += [g[:, j : j + lanes] for j in range(0, g.shape[1], lanes)]
    total = sum(b.shape[0] for b in blocks)
    devices = 1
    for stage in STAGES:
        devices *= lax.axis_size(stage)
    rows = -(-total // (devices * 16)) * devices * 16
    blocks.append(jnp.zeros((rows - total, lanes), jnp.float32))
    part = jnp.concatenate(blocks, 0).astype(jnp.bfloat16)
    for stage in STAGES:
        count = lax.axis_size(stage)
        got = lax.all_to_all(part, stage, 0, 0, tiled=True)
        part = got.reshape(count, -1, lanes).astype(jnp.float32).sum(0).astype(jnp.bfloat16)
    for stage in STAGES[::-1]:
        count = lax.axis_size(stage)
        spread = jnp.broadcast_to(part[None], (count,) + part.shape).reshape(-1, lanes)
        part = lax.all_to_all(spread, stage, 0, 0, tiled=True)
    out, start = [], 0
    for g in grads:
        height = g.shape[0] if g.ndim > 1 else 1
        pieces = []
        for _ in range(0, g.shape[-1], lanes):
            pieces.append(part[start : start + height])
            start += height + (-height % 16)
        out.append(jnp.concatenate(pieces, 1).astype(jnp.float32).reshape(g.shape))
    return out


def solution(mesh):
    space, group = mesh.shape["space"], mesh.shape["group"]
    sub = Mesh(
        mesh.devices.reshape(space // 8, 4, 2, group // 2, 2),
        ("zl", "x", "c", "y", "zh"),
    )
    S, G = SPACE, GROUP
    in_specs = (
        P(G, S, None),
        P(G, None, S),
        P(G, None),
        P(G, S),
        P(G, S, None),
        P(G, S, None),
        P(G, S, None),
        P(G, None, S),
        P(),
        P(),
        P(),
        P(),
        P(),
    )
    out_specs = (P(G, None, S), P(), P(), P(), P(), P())
    return jax.shard_map(
        per_device, mesh=sub, in_specs=in_specs, out_specs=out_specs, check_vma=False
    )
```

```python
import jax
import jax.numpy as jnp
from jax import lax
from jax.sharding import Mesh, PartitionSpec as P

RANGE_TOP = 48.0


def exchange(cells, dim, width):
    count = lax.axis_size(SPACE)
    head = lax.slice_in_dim(cells, 0, width, axis=dim)
    tail = lax.slice_in_dim(cells, cells.shape[dim] - width, cells.shape[dim], axis=dim)
    from_below = lax.ppermute(tail, SPACE, [(i, (i + 1) % count) for i in range(count)])
    from_above = lax.ppermute(head, SPACE, [((i + 1) % count, i) for i in range(count)])
    return from_below, from_above


def blocks_matrix(count, width):
    rows = lax.broadcasted_iota(jnp.int32, (count * width, width), 0)
    cols = lax.broadcasted_iota(jnp.int32, (count * width, width), 1)
    return (rows % width == cols).astype(jnp.float32)


def tiled(block, count):
    return jnp.dot(block, blocks_matrix(count, block.shape[1]).T, precision=lax.Precision.HIGHEST)


def block_sum(wide, width):
    return jnp.dot(wide, blocks_matrix(wide.shape[1] // width, width), precision=lax.Precision.HIGHEST)


def energy(params, table_feats, table_pos, neighbours, edge_mask, shift_ids, cell_box):
    w_zero, w_real, w_imag, radial, readout = params
    target_count, degree = neighbours.shape
    levels, channels = radial.shape
    flat_ids = neighbours.T.reshape(-1)
    shift_list = shift_ids.T.reshape(-1)
    live = edge_mask.T.reshape(-1)
    offset = (
        jnp.stack([shift_list // 9 - 1, shift_list // 3 % 3 - 1, shift_list % 3 - 1]).astype(
            jnp.float32
        )
        * cell_box[:, None]
    )
    edge_vec = (
        jnp.take(table_pos, flat_ids, axis=1)
        + offset
        - jnp.concatenate([table_pos[:, :target_count]] * degree, axis=1)
    )
    delta_one, delta_two, delta_three = (edge_vec[0], edge_vec[1], edge_vec[2])
    planar = jnp.sqrt(delta_one * delta_one + delta_two * delta_two + 1.0)
    radius = jnp.sqrt(planar * planar + delta_three * delta_three)
    cos_phi = (delta_one / planar)[:, None]
    sin_phi = (delta_two / planar)[:, None]
    cos_tilt = (delta_three / radius)[:, None]
    sin_tilt = (planar / radius)[:, None]
    spacing = RANGE_TOP / (levels - 1)
    centers = jnp.arange(levels, dtype=jnp.float32) * spacing
    basis_vals = jnp.exp(-jnp.square((radius[:, None] - centers[None, :]) / (2.0 * spacing)))
    radial_gain = jnp.dot(basis_vals, radial, precision=lax.Precision.HIGHEST)
    c = channels
    source = jnp.take(table_feats, flat_ids, axis=0).astype(jnp.float32)
    zero_part = source[:, 0 : 7 * c]
    plus_part = source[:, 7 * c : 13 * c]
    minus_part = source[:, 13 * c : 19 * c]
    plus_turn = cos_phi * plus_part + sin_phi * minus_part
    minus_turn = cos_phi * minus_part - sin_phi * plus_part
    upper = zero_part[:, c:]
    upper_tilt = cos_tilt * upper - sin_tilt * plus_turn
    plus_tilt = sin_tilt * upper + cos_tilt * plus_turn
    gain_six = tiled(radial_gain, 6)
    in_zero = (
        jnp.concatenate([zero_part[:, :c], upper_tilt], 1) * tiled(radial_gain, 7)
    ).astype(jnp.bfloat16)
    in_plus = (plus_tilt * gain_six).astype(jnp.bfloat16)
    in_minus = (minus_turn * gain_six).astype(jnp.bfloat16)
    weight_zero = w_zero.astype(jnp.bfloat16)
    weight_real = w_real.astype(jnp.bfloat16)
    weight_imag = w_imag.astype(jnp.bfloat16)
    out_zero = jnp.dot(in_zero, weight_zero, preferred_element_type=jnp.float32)
    out_plus = jnp.dot(in_plus, weight_real, preferred_element_type=jnp.float32) - jnp.dot(
        in_minus, weight_imag, preferred_element_type=jnp.float32
    )
    out_minus = jnp.dot(in_plus, weight_imag, preferred_element_type=jnp.float32) + jnp.dot(
        in_minus, weight_real, preferred_element_type=jnp.float32
    )
    zero_upper = out_zero[:, c:]
    upper_back = cos_tilt * zero_upper + sin_tilt * out_plus
    plus_back = cos_tilt * out_plus - sin_tilt * zero_upper
    plus_final = cos_phi * plus_back - sin_phi * out_minus
    minus_final = cos_phi * out_minus + sin_phi * plus_back
    message = jnp.concatenate([out_zero[:, :c], upper_back, plus_final, minus_final], 1)
    message = message * live.astype(jnp.float32)[:, None]
    summed = message[:target_count]
    for k in range(1, degree):
        summed = summed + message[k * target_count : (k + 1) * target_count]
    summed = summed / degree
    updated = table_feats[:target_count].astype(jnp.float32) + summed
    square = updated * updated
    total = block_sum(square, c)
    invariant = updated[:, :c] + total / 19
    return jnp.sum(jax.nn.silu(invariant) * readout[None, :])


def per_device(
    features,
    positions,
    cell_box,
    send_rows,
    neighbours,
    edge_mask,
    shift_ids,
    target_forces,
    w_zero,
    w_real,
    w_imag,
    radial,
    readout,
):
    atom_feats = features[0]
    atom_pos = positions[0]
    box_sides = cell_box[0]
    sends = send_rows[0]
    neighbour_ids = neighbours[0]
    edge_live = edge_mask[0]
    shift_list = shift_ids[0]
    wanted = target_forces[0]
    own_count = atom_feats.shape[0]
    ghosts = sends.shape[0] // 2
    part_count = lax.axis_size(SPACE)
    width = atom_feats.shape[1]
    listed = jnp.take(atom_feats, sends, axis=0).astype(jnp.float32)
    spots = jnp.take(atom_pos, sends, axis=1)
    lanes = -(-(width + 3) // 128) * 128
    both = jnp.concatenate(
        [listed, spots.T, jnp.zeros((listed.shape[0], lanes - width - 3), jnp.float32)], 1
    )
    below, above = exchange(both, 0, ghosts)
    table_feats = jnp.concatenate(
        [atom_feats, below[:, :width].astype(atom_feats.dtype), above[:, :width].astype(atom_feats.dtype)], 0
    )
    table_pos = jnp.concatenate(
        [atom_pos, below[:, width : width + 3].T, above[:, width : width + 3].T], 1
    )
    params = (
        w_zero.astype(jnp.float32),
        w_real.astype(jnp.float32),
        w_imag.astype(jnp.float32),
        radial,
        readout,
    )

    def position_grad(weights):
        return jax.grad(energy, 2)(
            weights, table_feats, table_pos, neighbour_ids, edge_live, shift_list, box_sides
        )

    grad_pos, pullback = jax.vjp(position_grad, params)
    ghost_grad = grad_pos[:, own_count:]
    returned = jnp.concatenate(exchange(ghost_grad, 1, ghosts), 1)
    onehot = (sends[:, None] == jnp.arange(own_count, dtype=jnp.int32)[None, :]).astype(jnp.float32)
    added = jnp.dot(returned, onehot, precision=lax.Precision.HIGHEST)
    forces = -(grad_pos[:, :own_count] + added)
    loss_weights = 2.0 * (forces - wanted) / (part_count * own_count)
    picked = jnp.take(loss_weights, sends, axis=1)
    table_u = jnp.concatenate([loss_weights, *exchange(picked, 1, ghosts)], 1)
    (grads,) = pullback(-table_u)
    grad_zero, grad_real, grad_imag, grad_radial, grad_readout = all_sum(grads)
    return (forces[None], grad_zero, grad_real, grad_imag, grad_radial, grad_readout)


SPACE = ("zl", "x", "c")
GROUP = ("y", "zh")
PAIR = "c"
STAGES = (("x", "y"), ("zh", "zl"))


def all_sum(grads):
    lanes = 128
    blocks = []
    for g in grads:
        g = g.reshape(-1, g.shape[-1]) if g.ndim > 1 else g.reshape(1, -1)
        g = jnp.pad(g, ((0, -g.shape[0] % 16), (0, 0)))
        blocks += [g[:, j : j + lanes] for j in range(0, g.shape[1], lanes)]
    total = sum(b.shape[0] for b in blocks)
    devices = lax.axis_size(PAIR)
    for stage in STAGES:
        devices *= lax.axis_size(stage)
    rows = -(-total // (devices * 16)) * devices * 16
    blocks.append(jnp.zeros((rows - total, lanes), jnp.float32))
    packed = jnp.concatenate(blocks, 0)
    core = lax.axis_index(PAIR)
    half = rows // 2
    mine = lax.dynamic_slice_in_dim(packed, core * half, half, 0)
    other = lax.dynamic_slice_in_dim(packed, (1 - core) * half, half, 0).astype(jnp.bfloat16)
    swap = [(0, 1), (1, 0)]
    part = (mine + lax.ppermute(other, PAIR, swap).astype(jnp.float32)).astype(jnp.bfloat16)
    for stage in STAGES:
        count = lax.axis_size(stage)
        got = lax.all_to_all(part, stage, 0, 0, tiled=True)
        part = got.reshape(count, -1, lanes).astype(jnp.float32).sum(0).astype(jnp.bfloat16)
    for stage in STAGES[::-1]:
        count = lax.axis_size(stage)
        spread = jnp.broadcast_to(part[None], (count,) + part.shape).reshape(-1, lanes)
        part = lax.all_to_all(spread, stage, 0, 0, tiled=True)
    got = lax.ppermute(part, PAIR, swap)
    part = jnp.where(core == 0, jnp.concatenate([part, got]), jnp.concatenate([got, part]))
    out, start = [], 0
    for g in grads:
        height = g.shape[0] if g.ndim > 1 else 1
        pieces = []
        for _ in range(0, g.shape[-1], lanes):
            pieces.append(part[start : start + height])
            start += height + (-height % 16)
        out.append(jnp.concatenate(pieces, 1).astype(jnp.float32).reshape(g.shape))
    return out


def solution(mesh):
    space, group = mesh.shape["space"], mesh.shape["group"]
    sub = Mesh(
        mesh.devices.reshape(space // 8, 4, 2, group // 2, 2),
        ("zl", "x", "c", "y", "zh"),
    )
    S, G = SPACE, GROUP
    in_specs = (
        P(G, S, None),
        P(G, None, S),
        P(G, None),
        P(G, S),
        P(G, S, None),
        P(G, S, None),
        P(G, S, None),
        P(G, None, S),
        P(),
        P(),
        P(),
        P(),
        P(),
    )
    out_specs = (P(G, None, S), P(), P(), P(), P(), P())
    return jax.shard_map(
        per_device, mesh=sub, in_specs=in_specs, out_specs=out_specs, check_vma=False
    )
```

```python
import jax
import jax.numpy as jnp
from jax import lax
from jax.sharding import Mesh, PartitionSpec as P

RANGE_TOP = 48.0


def exchange(cells, dim, width):
    count = lax.axis_size(SPACE)
    head = lax.slice_in_dim(cells, 0, width, axis=dim)
    tail = lax.slice_in_dim(cells, cells.shape[dim] - width, cells.shape[dim], axis=dim)
    from_below = lax.ppermute(tail, SPACE, [(i, (i + 1) % count) for i in range(count)])
    from_above = lax.ppermute(head, SPACE, [((i + 1) % count, i) for i in range(count)])
    return from_below, from_above


def blocks_matrix(count, width):
    rows = lax.broadcasted_iota(jnp.int32, (count * width, width), 0)
    cols = lax.broadcasted_iota(jnp.int32, (count * width, width), 1)
    return (rows % width == cols).astype(jnp.float32)


def tiled(block, count):
    return jnp.dot(block, blocks_matrix(count, block.shape[1]).T, precision=lax.Precision.HIGHEST)


def block_sum(wide, width):
    return jnp.dot(wide, blocks_matrix(wide.shape[1] // width, width), precision=lax.Precision.HIGHEST)


def energy(params, table_feats, table_pos, neighbours, edge_mask, shift_ids, cell_box):
    w_zero, w_real, w_imag, radial, readout = params
    target_count, degree = neighbours.shape
    levels, channels = radial.shape
    flat_ids = neighbours.T.reshape(-1)
    shift_list = shift_ids.T.reshape(-1)
    live = edge_mask.T.reshape(-1)
    offset = (
        jnp.stack([shift_list // 9 - 1, shift_list // 3 % 3 - 1, shift_list % 3 - 1]).astype(
            jnp.float32
        )
        * cell_box[:, None]
    )
    rows = lax.broadcasted_iota(jnp.int32, (table_pos.shape[1], flat_ids.shape[0]), 0)
    select = (rows == flat_ids[None, :]).astype(jnp.float32)
    edge_vec = (
        jnp.dot(table_pos, select, precision=lax.Precision.HIGHEST)
        + offset
        - jnp.concatenate([table_pos[:, :target_count]] * degree, axis=1)
    )
    delta_one, delta_two, delta_three = (edge_vec[0], edge_vec[1], edge_vec[2])
    planar = jnp.sqrt(delta_one * delta_one + delta_two * delta_two + 1.0)
    radius = jnp.sqrt(planar * planar + delta_three * delta_three)
    cos_phi = (delta_one / planar)[:, None]
    sin_phi = (delta_two / planar)[:, None]
    cos_tilt = (delta_three / radius)[:, None]
    sin_tilt = (planar / radius)[:, None]
    spacing = RANGE_TOP / (levels - 1)
    centers = jnp.arange(levels, dtype=jnp.float32) * spacing
    basis_vals = jnp.exp(-jnp.square((radius[:, None] - centers[None, :]) / (2.0 * spacing)))
    radial_gain = jnp.dot(basis_vals, radial, precision=lax.Precision.HIGHEST)
    c = channels
    source = jnp.dot(
        select.T.astype(table_feats.dtype), table_feats, preferred_element_type=jnp.float32
    )
    zero_part = source[:, 0 : 7 * c]
    plus_part = source[:, 7 * c : 13 * c]
    minus_part = source[:, 13 * c : 19 * c]
    plus_turn = cos_phi * plus_part + sin_phi * minus_part
    minus_turn = cos_phi * minus_part - sin_phi * plus_part
    upper = zero_part[:, c:]
    upper_tilt = cos_tilt * upper - sin_tilt * plus_turn
    plus_tilt = sin_tilt * upper + cos_tilt * plus_turn
    gain_six = tiled(radial_gain, 6)
    in_zero = (
        jnp.concatenate([zero_part[:, :c], upper_tilt], 1) * tiled(radial_gain, 7)
    ).astype(jnp.bfloat16)
    in_plus = (plus_tilt * gain_six).astype(jnp.bfloat16)
    in_minus = (minus_turn * gain_six).astype(jnp.bfloat16)
    weight_zero = w_zero.astype(jnp.bfloat16)
    weight_real = w_real.astype(jnp.bfloat16)
    weight_imag = w_imag.astype(jnp.bfloat16)
    out_zero = jnp.dot(in_zero, weight_zero, preferred_element_type=jnp.float32)
    out_plus = jnp.dot(in_plus, weight_real, preferred_element_type=jnp.float32) - jnp.dot(
        in_minus, weight_imag, preferred_element_type=jnp.float32
    )
    out_minus = jnp.dot(in_plus, weight_imag, preferred_element_type=jnp.float32) + jnp.dot(
        in_minus, weight_real, preferred_element_type=jnp.float32
    )
    zero_upper = out_zero[:, c:]
    upper_back = cos_tilt * zero_upper + sin_tilt * out_plus
    plus_back = cos_tilt * out_plus - sin_tilt * zero_upper
    plus_final = cos_phi * plus_back - sin_phi * out_minus
    minus_final = cos_phi * out_minus + sin_phi * plus_back
    message = jnp.concatenate([out_zero[:, :c], upper_back, plus_final, minus_final], 1)
    message = message * live.astype(jnp.float32)[:, None]
    summed = message[:target_count]
    for k in range(1, degree):
        summed = summed + message[k * target_count : (k + 1) * target_count]
    summed = summed / degree
    updated = table_feats[:target_count].astype(jnp.float32) + summed
    square = updated * updated
    total = block_sum(square, c)
    invariant = updated[:, :c] + total / 19
    return jnp.sum(jax.nn.silu(invariant) * readout[None, :])


def per_device(
    features,
    positions,
    cell_box,
    send_rows,
    neighbours,
    edge_mask,
    shift_ids,
    target_forces,
    w_zero,
    w_real,
    w_imag,
    radial,
    readout,
):
    atom_feats = features[0]
    atom_pos = positions[0]
    box_sides = cell_box[0]
    sends = send_rows[0]
    neighbour_ids = neighbours[0]
    edge_live = edge_mask[0]
    shift_list = shift_ids[0]
    wanted = target_forces[0]
    own_count = atom_feats.shape[0]
    ghosts = sends.shape[0] // 2
    part_count = lax.axis_size(SPACE)
    width = atom_feats.shape[1]
    listed = jnp.take(atom_feats, sends, axis=0).astype(jnp.float32)
    spots = jnp.take(atom_pos, sends, axis=1)
    lanes = -(-(width + 3) // 128) * 128
    both = jnp.concatenate(
        [listed, spots.T, jnp.zeros((listed.shape[0], lanes - width - 3), jnp.float32)], 1
    )
    below, above = exchange(both, 0, ghosts)
    table_feats = jnp.concatenate(
        [atom_feats, below[:, :width].astype(atom_feats.dtype), above[:, :width].astype(atom_feats.dtype)], 0
    )
    table_pos = jnp.concatenate(
        [atom_pos, below[:, width : width + 3].T, above[:, width : width + 3].T], 1
    )
    params = (
        w_zero.astype(jnp.float32),
        w_real.astype(jnp.float32),
        w_imag.astype(jnp.float32),
        radial,
        readout,
    )

    def position_grad(weights):
        return jax.grad(energy, 2)(
            weights, table_feats, table_pos, neighbour_ids, edge_live, shift_list, box_sides
        )

    grad_pos, pullback = jax.vjp(position_grad, params)
    ghost_grad = grad_pos[:, own_count:]
    returned = jnp.concatenate(exchange(ghost_grad, 1, ghosts), 1)
    onehot = (sends[:, None] == jnp.arange(own_count, dtype=jnp.int32)[None, :]).astype(jnp.float32)
    added = jnp.dot(returned, onehot, precision=lax.Precision.HIGHEST)
    forces = -(grad_pos[:, :own_count] + added)
    loss_weights = 2.0 * (forces - wanted) / (part_count * own_count)
    picked = jnp.take(loss_weights, sends, axis=1)
    table_u = jnp.concatenate([loss_weights, *exchange(picked, 1, ghosts)], 1)
    (grads,) = pullback(-table_u)
    grad_zero, grad_real, grad_imag, grad_radial, grad_readout = all_sum(grads)
    return (forces[None], grad_zero, grad_real, grad_imag, grad_radial, grad_readout)


SPACE = ("zl", "x", "c")
GROUP = ("y", "zh")
STAGES = (("c",), ("x", "y"), ("zh", "zl"))


def all_sum(grads):
    lanes = 128
    blocks = []
    for g in grads:
        g = g.reshape(-1, g.shape[-1]) if g.ndim > 1 else g.reshape(1, -1)
        g = jnp.pad(g, ((0, -g.shape[0] % 16), (0, 0)))
        blocks += [g[:, j : j + lanes] for j in range(0, g.shape[1], lanes)]
    total = sum(b.shape[0] for b in blocks)
    devices = 1
    for stage in STAGES:
        devices *= lax.axis_size(stage)
    rows = -(-total // (devices * 16)) * devices * 16
    blocks.append(jnp.zeros((rows - total, lanes), jnp.float32))
    part = jnp.concatenate(blocks, 0).astype(jnp.bfloat16)
    for stage in STAGES:
        count = lax.axis_size(stage)
        got = lax.all_to_all(part, stage, 0, 0, tiled=True)
        part = got.reshape(count, -1, lanes).astype(jnp.float32).sum(0).astype(jnp.bfloat16)
    for stage in STAGES[::-1]:
        count = lax.axis_size(stage)
        spread = jnp.broadcast_to(part[None], (count,) + part.shape).reshape(-1, lanes)
        part = lax.all_to_all(spread, stage, 0, 0, tiled=True)
    out, start = [], 0
    for g in grads:
        height = g.shape[0] if g.ndim > 1 else 1
        pieces = []
        for _ in range(0, g.shape[-1], lanes):
            pieces.append(part[start : start + height])
            start += height + (-height % 16)
        out.append(jnp.concatenate(pieces, 1).astype(jnp.float32).reshape(g.shape))
    return out


def solution(mesh):
    space, group = mesh.shape["space"], mesh.shape["group"]
    sub = Mesh(
        mesh.devices.reshape(space // 8, 4, 2, group // 2, 2),
        ("zl", "x", "c", "y", "zh"),
    )
    S, G = SPACE, GROUP
    in_specs = (
        P(G, S, None),
        P(G, None, S),
        P(G, None),
        P(G, S),
        P(G, S, None),
        P(G, S, None),
        P(G, S, None),
        P(G, None, S),
        P(),
        P(),
        P(),
        P(),
        P(),
    )
    out_specs = (P(G, None, S), P(), P(), P(), P(), P())
    return jax.shard_map(
        per_device, mesh=sub, in_specs=in_specs, out_specs=out_specs, check_vma=False
    )
```

```python
import jax
import jax.numpy as jnp
from jax import lax
from jax.sharding import Mesh, PartitionSpec as P

RANGE_TOP = 48.0


def exchange(cells, dim, width):
    count = lax.axis_size(SPACE)
    head = lax.slice_in_dim(cells, 0, width, axis=dim)
    tail = lax.slice_in_dim(cells, cells.shape[dim] - width, cells.shape[dim], axis=dim)
    from_below = lax.ppermute(tail, SPACE, [(i, (i + 1) % count) for i in range(count)])
    from_above = lax.ppermute(head, SPACE, [((i + 1) % count, i) for i in range(count)])
    return from_below, from_above


def blocks_matrix(count, width):
    rows = lax.broadcasted_iota(jnp.int32, (count * width, width), 0)
    cols = lax.broadcasted_iota(jnp.int32, (count * width, width), 1)
    return (rows % width == cols).astype(jnp.float32)


def tiled(block, count):
    return jnp.dot(block, blocks_matrix(count, block.shape[1]).T, precision=lax.Precision.HIGHEST)


def block_sum(wide, width):
    return jnp.dot(wide, blocks_matrix(wide.shape[1] // width, width), precision=lax.Precision.HIGHEST)


def energy(params, table_feats, table_pos, neighbours, edge_mask, shift_ids, cell_box):
    w_zero, w_real, w_imag, radial, readout = params
    target_count, degree = neighbours.shape
    levels, channels = radial.shape
    flat_ids = neighbours.T.reshape(-1)
    shift_list = shift_ids.T.reshape(-1)
    live = edge_mask.T.reshape(-1)
    offset = (
        jnp.stack([shift_list // 9 - 1, shift_list // 3 % 3 - 1, shift_list % 3 - 1]).astype(
            jnp.float32
        )
        * cell_box[:, None]
    )
    rows = lax.broadcasted_iota(jnp.int32, (table_pos.shape[1], flat_ids.shape[0]), 0)
    select = (rows == flat_ids[None, :]).astype(jnp.float32)
    edge_vec = (
        jnp.dot(table_pos, select, precision=lax.Precision.HIGHEST)
        + offset
        - jnp.concatenate([table_pos[:, :target_count]] * degree, axis=1)
    )
    delta_one, delta_two, delta_three = (edge_vec[0], edge_vec[1], edge_vec[2])
    planar = jnp.sqrt(delta_one * delta_one + delta_two * delta_two + 1.0)
    radius = jnp.sqrt(planar * planar + delta_three * delta_three)
    cos_phi = (delta_one / planar)[:, None]
    sin_phi = (delta_two / planar)[:, None]
    cos_tilt = (delta_three / radius)[:, None]
    sin_tilt = (planar / radius)[:, None]
    spacing = RANGE_TOP / (levels - 1)
    centers = jnp.arange(levels, dtype=jnp.float32) * spacing
    basis_vals = jnp.exp(-jnp.square((radius[:, None] - centers[None, :]) / (2.0 * spacing)))
    radial_gain = jnp.dot(basis_vals, radial, precision=lax.Precision.HIGHEST)
    c = channels
    source = jnp.dot(
        select.T.astype(table_feats.dtype), table_feats, preferred_element_type=jnp.float32
    )
    zero_part = source[:, 0 : 7 * c]
    plus_part = source[:, 7 * c : 13 * c]
    minus_part = source[:, 13 * c : 19 * c]
    plus_turn = cos_phi * plus_part + sin_phi * minus_part
    minus_turn = cos_phi * minus_part - sin_phi * plus_part
    upper = zero_part[:, c:]
    upper_tilt = cos_tilt * upper - sin_tilt * plus_turn
    plus_tilt = sin_tilt * upper + cos_tilt * plus_turn
    gain_six = tiled(radial_gain, 6)
    in_zero = (
        jnp.concatenate([zero_part[:, :c], upper_tilt], 1) * tiled(radial_gain, 7)
    ).astype(jnp.bfloat16)
    in_plus = (plus_tilt * gain_six).astype(jnp.bfloat16)
    in_minus = (minus_turn * gain_six).astype(jnp.bfloat16)
    weight_zero = w_zero.astype(jnp.bfloat16)
    weight_real = w_real.astype(jnp.bfloat16)
    weight_imag = w_imag.astype(jnp.bfloat16)
    out_zero = jnp.dot(in_zero, weight_zero, preferred_element_type=jnp.float32)
    out_plus = jnp.dot(in_plus, weight_real, preferred_element_type=jnp.float32) - jnp.dot(
        in_minus, weight_imag, preferred_element_type=jnp.float32
    )
    out_minus = jnp.dot(in_plus, weight_imag, preferred_element_type=jnp.float32) + jnp.dot(
        in_minus, weight_real, preferred_element_type=jnp.float32
    )
    zero_upper = out_zero[:, c:]
    upper_back = cos_tilt * zero_upper + sin_tilt * out_plus
    plus_back = cos_tilt * out_plus - sin_tilt * zero_upper
    plus_final = cos_phi * plus_back - sin_phi * out_minus
    minus_final = cos_phi * out_minus + sin_phi * plus_back
    message = jnp.concatenate([out_zero[:, :c], upper_back, plus_final, minus_final], 1)
    message = message * live.astype(jnp.float32)[:, None]
    summed = message[:target_count]
    for k in range(1, degree):
        summed = summed + message[k * target_count : (k + 1) * target_count]
    summed = summed / degree
    updated = table_feats[:target_count].astype(jnp.float32) + summed
    square = updated * updated
    total = block_sum(square, c)
    invariant = updated[:, :c] + total / 19
    return jnp.sum(jax.nn.silu(invariant) * readout[None, :])


def per_device(
    features,
    positions,
    cell_box,
    send_rows,
    neighbours,
    edge_mask,
    shift_ids,
    target_forces,
    w_zero,
    w_real,
    w_imag,
    radial,
    readout,
):
    atom_feats = features[0]
    atom_pos = positions[0]
    box_sides = cell_box[0]
    sends = send_rows[0]
    neighbour_ids = neighbours[0]
    edge_live = edge_mask[0]
    shift_list = shift_ids[0]
    wanted = target_forces[0]
    own_count = atom_feats.shape[0]
    ghosts = sends.shape[0] // 2
    part_count = lax.axis_size(SPACE)
    width = atom_feats.shape[1]
    onehot = (sends[:, None] == jnp.arange(own_count, dtype=jnp.int32)[None, :]).astype(jnp.float32)
    listed = jnp.dot(onehot.astype(atom_feats.dtype), atom_feats, preferred_element_type=jnp.float32)
    spots = jnp.dot(atom_pos, onehot.T, precision=lax.Precision.HIGHEST)
    lanes = -(-(width + 3) // 128) * 128
    both = jnp.concatenate(
        [listed, spots.T, jnp.zeros((listed.shape[0], lanes - width - 3), jnp.float32)], 1
    )
    below, above = exchange(both, 0, ghosts)
    table_feats = jnp.concatenate(
        [atom_feats, below[:, :width].astype(atom_feats.dtype), above[:, :width].astype(atom_feats.dtype)], 0
    )
    table_pos = jnp.concatenate(
        [atom_pos, below[:, width : width + 3].T, above[:, width : width + 3].T], 1
    )
    params = (
        w_zero.astype(jnp.float32),
        w_real.astype(jnp.float32),
        w_imag.astype(jnp.float32),
        radial,
        readout,
    )

    def position_grad(weights):
        return jax.grad(energy, 2)(
            weights, table_feats, table_pos, neighbour_ids, edge_live, shift_list, box_sides
        )

    grad_pos, pullback = jax.vjp(position_grad, params)
    ghost_grad = grad_pos[:, own_count:]
    returned = jnp.concatenate(exchange(ghost_grad, 1, ghosts), 1)
    added = jnp.dot(returned, onehot, precision=lax.Precision.HIGHEST)
    forces = -(grad_pos[:, :own_count] + added)
    loss_weights = 2.0 * (forces - wanted) / (part_count * own_count)
    picked = jnp.dot(loss_weights, onehot.T, precision=lax.Precision.HIGHEST)
    table_u = jnp.concatenate([loss_weights, *exchange(picked, 1, ghosts)], 1)
    (grads,) = pullback(-table_u)
    grad_zero, grad_real, grad_imag, grad_radial, grad_readout = all_sum(grads)
    return (forces[None], grad_zero, grad_real, grad_imag, grad_radial, grad_readout)


SPACE = ("zl", "x", "c")
GROUP = ("y", "zh")
STAGES = (("c",), ("x", "y"), ("zh", "zl"))


def all_sum(grads):
    lanes = 128
    blocks = []
    for g in grads:
        g = g.reshape(-1, g.shape[-1]) if g.ndim > 1 else g.reshape(1, -1)
        g = jnp.pad(g, ((0, -g.shape[0] % 16), (0, 0)))
        blocks += [g[:, j : j + lanes] for j in range(0, g.shape[1], lanes)]
    total = sum(b.shape[0] for b in blocks)
    devices = 1
    for stage in STAGES:
        devices *= lax.axis_size(stage)
    rows = -(-total // (devices * 16)) * devices * 16
    blocks.append(jnp.zeros((rows - total, lanes), jnp.float32))
    part = jnp.concatenate(blocks, 0).astype(jnp.bfloat16)
    for stage in STAGES:
        count = lax.axis_size(stage)
        got = lax.all_to_all(part, stage, 0, 0, tiled=True)
        part = got.reshape(count, -1, lanes).astype(jnp.float32).sum(0).astype(jnp.bfloat16)
    for stage in STAGES[::-1]:
        count = lax.axis_size(stage)
        spread = jnp.broadcast_to(part[None], (count,) + part.shape).reshape(-1, lanes)
        part = lax.all_to_all(spread, stage, 0, 0, tiled=True)
    out, start = [], 0
    for g in grads:
        height = g.shape[0] if g.ndim > 1 else 1
        pieces = []
        for _ in range(0, g.shape[-1], lanes):
            pieces.append(part[start : start + height])
            start += height + (-height % 16)
        out.append(jnp.concatenate(pieces, 1).astype(jnp.float32).reshape(g.shape))
    return out


def solution(mesh):
    space, group = mesh.shape["space"], mesh.shape["group"]
    sub = Mesh(
        mesh.devices.reshape(space // 8, 4, 2, group // 2, 2),
        ("zl", "x", "c", "y", "zh"),
    )
    S, G = SPACE, GROUP
    in_specs = (
        P(G, S, None),
        P(G, None, S),
        P(G, None),
        P(G, S),
        P(G, S, None),
        P(G, S, None),
        P(G, S, None),
        P(G, None, S),
        P(),
        P(),
        P(),
        P(),
        P(),
    )
    out_specs = (P(G, None, S), P(), P(), P(), P(), P())
    return jax.shard_map(
        per_device, mesh=sub, in_specs=in_specs, out_specs=out_specs, check_vma=False
    )
```

```python
import jax
import jax.numpy as jnp
from jax import lax
from jax.sharding import Mesh, PartitionSpec as P

RANGE_TOP = 48.0


def exchange(cells, dim, width):
    count = lax.axis_size(SPACE)
    head = lax.slice_in_dim(cells, 0, width, axis=dim)
    tail = lax.slice_in_dim(cells, cells.shape[dim] - width, cells.shape[dim], axis=dim)
    from_below = lax.ppermute(tail, SPACE, [(i, (i + 1) % count) for i in range(count)])
    from_above = lax.ppermute(head, SPACE, [((i + 1) % count, i) for i in range(count)])
    return from_below, from_above


def blocks_matrix(count, width):
    rows = lax.broadcasted_iota(jnp.int32, (count * width, width), 0)
    cols = lax.broadcasted_iota(jnp.int32, (count * width, width), 1)
    return (rows % width == cols).astype(jnp.float32)


def tiled(block, count):
    return jnp.dot(block, blocks_matrix(count, block.shape[1]).T, precision=lax.Precision.HIGH)


def block_sum(wide, width):
    return jnp.dot(wide, blocks_matrix(wide.shape[1] // width, width), precision=lax.Precision.HIGH)


def energy(params, table_feats, table_pos, neighbours, edge_mask, shift_ids, cell_box):
    w_zero, w_real, w_imag, radial, readout = params
    target_count, degree = neighbours.shape
    levels, channels = radial.shape
    flat_ids = neighbours.T.reshape(-1)
    shift_list = shift_ids.T.reshape(-1)
    live = edge_mask.T.reshape(-1)
    offset = (
        jnp.stack([shift_list // 9 - 1, shift_list // 3 % 3 - 1, shift_list % 3 - 1]).astype(
            jnp.float32
        )
        * cell_box[:, None]
    )
    rows = lax.broadcasted_iota(jnp.int32, (table_pos.shape[1], flat_ids.shape[0]), 0)
    select = (rows == flat_ids[None, :]).astype(jnp.float32)
    edge_vec = (
        jnp.dot(table_pos, select, precision=lax.Precision.HIGHEST)
        + offset
        - jnp.concatenate([table_pos[:, :target_count]] * degree, axis=1)
    )
    delta_one, delta_two, delta_three = (edge_vec[0], edge_vec[1], edge_vec[2])
    planar = jnp.sqrt(delta_one * delta_one + delta_two * delta_two + 1.0)
    radius = jnp.sqrt(planar * planar + delta_three * delta_three)
    cos_phi = (delta_one / planar)[:, None]
    sin_phi = (delta_two / planar)[:, None]
    cos_tilt = (delta_three / radius)[:, None]
    sin_tilt = (planar / radius)[:, None]
    spacing = RANGE_TOP / (levels - 1)
    centers = jnp.arange(levels, dtype=jnp.float32) * spacing
    basis_vals = jnp.exp(-jnp.square((radius[:, None] - centers[None, :]) / (2.0 * spacing)))
    radial_gain = jnp.dot(basis_vals, radial, precision=lax.Precision.HIGHEST)
    c = channels
    source = jnp.dot(
        select.T.astype(table_feats.dtype), table_feats, preferred_element_type=jnp.float32
    )
    zero_part = source[:, 0 : 7 * c]
    plus_part = source[:, 7 * c : 13 * c]
    minus_part = source[:, 13 * c : 19 * c]
    plus_turn = cos_phi * plus_part + sin_phi * minus_part
    minus_turn = cos_phi * minus_part - sin_phi * plus_part
    upper = zero_part[:, c:]
    upper_tilt = cos_tilt * upper - sin_tilt * plus_turn
    plus_tilt = sin_tilt * upper + cos_tilt * plus_turn
    gain_six = tiled(radial_gain, 6)
    in_zero = (
        jnp.concatenate([zero_part[:, :c], upper_tilt], 1) * tiled(radial_gain, 7)
    ).astype(jnp.bfloat16)
    in_plus = (plus_tilt * gain_six).astype(jnp.bfloat16)
    in_minus = (minus_turn * gain_six).astype(jnp.bfloat16)
    weight_zero = w_zero.astype(jnp.bfloat16)
    weight_real = w_real.astype(jnp.bfloat16)
    weight_imag = w_imag.astype(jnp.bfloat16)
    out_zero = jnp.dot(in_zero, weight_zero, preferred_element_type=jnp.float32)
    out_plus = jnp.dot(in_plus, weight_real, preferred_element_type=jnp.float32) - jnp.dot(
        in_minus, weight_imag, preferred_element_type=jnp.float32
    )
    out_minus = jnp.dot(in_plus, weight_imag, preferred_element_type=jnp.float32) + jnp.dot(
        in_minus, weight_real, preferred_element_type=jnp.float32
    )
    zero_upper = out_zero[:, c:]
    upper_back = cos_tilt * zero_upper + sin_tilt * out_plus
    plus_back = cos_tilt * out_plus - sin_tilt * zero_upper
    plus_final = cos_phi * plus_back - sin_phi * out_minus
    minus_final = cos_phi * out_minus + sin_phi * plus_back
    message = jnp.concatenate([out_zero[:, :c], upper_back, plus_final, minus_final], 1)
    message = message * live.astype(jnp.float32)[:, None]
    summed = message[:target_count]
    for k in range(1, degree):
        summed = summed + message[k * target_count : (k + 1) * target_count]
    summed = summed / degree
    updated = table_feats[:target_count].astype(jnp.float32) + summed
    square = updated * updated
    total = block_sum(square, c)
    invariant = updated[:, :c] + total / 19
    return jnp.sum(jax.nn.silu(invariant) * readout[None, :])


def per_device(
    features,
    positions,
    cell_box,
    send_rows,
    neighbours,
    edge_mask,
    shift_ids,
    target_forces,
    w_zero,
    w_real,
    w_imag,
    radial,
    readout,
):
    atom_feats = features[0]
    atom_pos = positions[0]
    box_sides = cell_box[0]
    sends = send_rows[0]
    neighbour_ids = neighbours[0]
    edge_live = edge_mask[0]
    shift_list = shift_ids[0]
    wanted = target_forces[0]
    own_count = atom_feats.shape[0]
    ghosts = sends.shape[0] // 2
    part_count = lax.axis_size(SPACE)
    width = atom_feats.shape[1]
    onehot = (sends[:, None] == jnp.arange(own_count, dtype=jnp.int32)[None, :]).astype(jnp.float32)
    listed = jnp.dot(onehot.astype(atom_feats.dtype), atom_feats, preferred_element_type=jnp.float32)
    spots = jnp.dot(atom_pos, onehot.T, precision=lax.Precision.HIGHEST)
    lanes = -(-(width + 3) // 128) * 128
    both = jnp.concatenate(
        [listed, spots.T, jnp.zeros((listed.shape[0], lanes - width - 3), jnp.float32)], 1
    )
    below, above = exchange(both, 0, ghosts)
    table_feats = jnp.concatenate(
        [atom_feats, below[:, :width].astype(atom_feats.dtype), above[:, :width].astype(atom_feats.dtype)], 0
    )
    table_pos = jnp.concatenate(
        [atom_pos, below[:, width : width + 3].T, above[:, width : width + 3].T], 1
    )
    params = (
        w_zero.astype(jnp.float32),
        w_real.astype(jnp.float32),
        w_imag.astype(jnp.float32),
        radial,
        readout,
    )

    def position_grad(weights):
        return jax.grad(energy, 2)(
            weights, table_feats, table_pos, neighbour_ids, edge_live, shift_list, box_sides
        )

    grad_pos, pullback = jax.vjp(position_grad, params)
    ghost_grad = grad_pos[:, own_count:]
    returned = jnp.concatenate(exchange(ghost_grad, 1, ghosts), 1)
    added = jnp.dot(returned, onehot, precision=lax.Precision.HIGHEST)
    forces = -(grad_pos[:, :own_count] + added)
    loss_weights = 2.0 * (forces - wanted) / (part_count * own_count)
    picked = jnp.dot(loss_weights, onehot.T, precision=lax.Precision.HIGHEST)
    table_u = jnp.concatenate([loss_weights, *exchange(picked, 1, ghosts)], 1)
    (grads,) = pullback(-table_u)
    grad_zero, grad_real, grad_imag, grad_radial, grad_readout = all_sum(grads)
    return (forces[None], grad_zero, grad_real, grad_imag, grad_radial, grad_readout)


SPACE = ("zl", "x", "c")
GROUP = ("y", "zh")
STAGES = (("c",), ("x", "y"), ("zh", "zl"))


def all_sum(grads):
    lanes = 128
    blocks = []
    for g in grads:
        g = g.reshape(-1, g.shape[-1]) if g.ndim > 1 else g.reshape(1, -1)
        g = jnp.pad(g, ((0, -g.shape[0] % 16), (0, 0)))
        blocks += [g[:, j : j + lanes] for j in range(0, g.shape[1], lanes)]
    total = sum(b.shape[0] for b in blocks)
    devices = 1
    for stage in STAGES:
        devices *= lax.axis_size(stage)
    rows = -(-total // (devices * 16)) * devices * 16
    blocks.append(jnp.zeros((rows - total, lanes), jnp.float32))
    part = jnp.concatenate(blocks, 0).astype(jnp.bfloat16)
    for stage in STAGES:
        count = lax.axis_size(stage)
        got = lax.all_to_all(part, stage, 0, 0, tiled=True)
        part = got.reshape(count, -1, lanes).astype(jnp.float32).sum(0).astype(jnp.bfloat16)
    for stage in STAGES[::-1]:
        count = lax.axis_size(stage)
        spread = jnp.broadcast_to(part[None], (count,) + part.shape).reshape(-1, lanes)
        part = lax.all_to_all(spread, stage, 0, 0, tiled=True)
    out, start = [], 0
    for g in grads:
        height = g.shape[0] if g.ndim > 1 else 1
        pieces = []
        for _ in range(0, g.shape[-1], lanes):
            pieces.append(part[start : start + height])
            start += height + (-height % 16)
        out.append(jnp.concatenate(pieces, 1).astype(jnp.float32).reshape(g.shape))
    return out


def solution(mesh):
    space, group = mesh.shape["space"], mesh.shape["group"]
    sub = Mesh(
        mesh.devices.reshape(space // 8, 4, 2, group // 2, 2),
        ("zl", "x", "c", "y", "zh"),
    )
    S, G = SPACE, GROUP
    in_specs = (
        P(G, S, None),
        P(G, None, S),
        P(G, None),
        P(G, S),
        P(G, S, None),
        P(G, S, None),
        P(G, S, None),
        P(G, None, S),
        P(),
        P(),
        P(),
        P(),
        P(),
    )
    out_specs = (P(G, None, S), P(), P(), P(), P(), P())
    return jax.shard_map(
        per_device, mesh=sub, in_specs=in_specs, out_specs=out_specs, check_vma=False
    )
```

```python
import jax
import jax.numpy as jnp
from jax import lax
from jax.sharding import Mesh, PartitionSpec as P

RANGE_TOP = 48.0


def exchange(cells, dim, width):
    count = lax.axis_size(SPACE)
    head = lax.slice_in_dim(cells, 0, width, axis=dim)
    tail = lax.slice_in_dim(cells, cells.shape[dim] - width, cells.shape[dim], axis=dim)
    from_below = lax.ppermute(tail, SPACE, [(i, (i + 1) % count) for i in range(count)])
    from_above = lax.ppermute(head, SPACE, [((i + 1) % count, i) for i in range(count)])
    return from_below, from_above


def blocks_matrix(count, width):
    rows = lax.broadcasted_iota(jnp.int32, (count * width, width), 0)
    cols = lax.broadcasted_iota(jnp.int32, (count * width, width), 1)
    return (rows % width == cols).astype(jnp.float32)


def tiled(block, count):
    return jnp.dot(block, blocks_matrix(count, block.shape[1]).T, precision=lax.Precision.HIGH)


def block_sum(wide, width):
    return jnp.dot(wide, blocks_matrix(wide.shape[1] // width, width), precision=lax.Precision.HIGH)


def energy(params, table_feats, table_pos, neighbours, edge_mask, shift_ids, cell_box):
    w_zero, w_real, w_imag, radial, readout = params
    target_count, degree = neighbours.shape
    levels, channels = radial.shape
    flat_ids = neighbours.T.reshape(-1)
    shift_list = shift_ids.T.reshape(-1)
    live = edge_mask.T.reshape(-1)
    offset = (
        jnp.stack([shift_list // 9 - 1, shift_list // 3 % 3 - 1, shift_list % 3 - 1]).astype(
            jnp.float32
        )
        * cell_box[:, None]
    )
    rows = lax.broadcasted_iota(jnp.int32, (table_pos.shape[1], flat_ids.shape[0]), 0)
    select = (rows == flat_ids[None, :]).astype(jnp.float32)
    edge_vec = (
        jnp.dot(table_pos, select, precision=lax.Precision.HIGHEST)
        + offset
        - jnp.concatenate([table_pos[:, :target_count]] * degree, axis=1)
    )
    delta_one, delta_two, delta_three = (edge_vec[0], edge_vec[1], edge_vec[2])
    planar = jnp.sqrt(delta_one * delta_one + delta_two * delta_two + 1.0)
    radius = jnp.sqrt(planar * planar + delta_three * delta_three)
    cos_phi = (delta_one / planar)[:, None]
    sin_phi = (delta_two / planar)[:, None]
    cos_tilt = (delta_three / radius)[:, None]
    sin_tilt = (planar / radius)[:, None]
    spacing = RANGE_TOP / (levels - 1)
    centers = jnp.arange(levels, dtype=jnp.float32) * spacing
    basis_vals = jnp.exp(-jnp.square((radius[:, None] - centers[None, :]) / (2.0 * spacing)))
    radial_gain = jnp.dot(basis_vals, radial, precision=lax.Precision.HIGHEST)
    c = channels
    source = jnp.dot(
        select.T.astype(table_feats.dtype), table_feats, preferred_element_type=jnp.float32
    )
    zero_part = source[:, 0 : 7 * c]
    plus_part = source[:, 7 * c : 13 * c]
    minus_part = source[:, 13 * c : 19 * c]
    plus_turn = cos_phi * plus_part + sin_phi * minus_part
    minus_turn = cos_phi * minus_part - sin_phi * plus_part
    upper = zero_part[:, c:]
    upper_tilt = cos_tilt * upper - sin_tilt * plus_turn
    plus_tilt = sin_tilt * upper + cos_tilt * plus_turn
    gain_six = tiled(radial_gain, 6)
    in_zero = (
        jnp.concatenate([zero_part[:, :c], upper_tilt], 1) * tiled(radial_gain, 7)
    ).astype(jnp.bfloat16)
    in_plus = (plus_tilt * gain_six).astype(jnp.bfloat16)
    in_minus = (minus_turn * gain_six).astype(jnp.bfloat16)
    weight_zero = w_zero.astype(jnp.bfloat16)
    weight_real = w_real.astype(jnp.bfloat16)
    weight_imag = w_imag.astype(jnp.bfloat16)
    out_zero = jnp.dot(in_zero, weight_zero, preferred_element_type=jnp.float32)
    out_plus = jnp.dot(in_plus, weight_real, preferred_element_type=jnp.float32) - jnp.dot(
        in_minus, weight_imag, preferred_element_type=jnp.float32
    )
    out_minus = jnp.dot(in_plus, weight_imag, preferred_element_type=jnp.float32) + jnp.dot(
        in_minus, weight_real, preferred_element_type=jnp.float32
    )
    zero_upper = out_zero[:, c:]
    upper_back = cos_tilt * zero_upper + sin_tilt * out_plus
    plus_back = cos_tilt * out_plus - sin_tilt * zero_upper
    plus_final = cos_phi * plus_back - sin_phi * out_minus
    minus_final = cos_phi * out_minus + sin_phi * plus_back
    message = jnp.concatenate([out_zero[:, :c], upper_back, plus_final, minus_final], 1)
    message = message * live.astype(jnp.float32)[:, None]
    summed = message[:target_count]
    for k in range(1, degree):
        summed = summed + message[k * target_count : (k + 1) * target_count]
    summed = summed / degree
    updated = table_feats[:target_count].astype(jnp.float32) + summed
    square = updated * updated
    total = block_sum(square, c)
    invariant = updated[:, :c] + total / 19
    return jnp.sum(jax.nn.silu(invariant) * readout[None, :])


def per_device(
    features,
    positions,
    cell_box,
    send_rows,
    neighbours,
    edge_mask,
    shift_ids,
    target_forces,
    w_zero,
    w_real,
    w_imag,
    radial,
    readout,
):
    atom_feats = features[0]
    atom_pos = positions[0]
    box_sides = cell_box[0]
    sends = send_rows[0]
    neighbour_ids = neighbours[0]
    edge_live = edge_mask[0]
    shift_list = shift_ids[0]
    wanted = target_forces[0]
    own_count = atom_feats.shape[0]
    ghosts = sends.shape[0] // 2
    part_count = lax.axis_size(SPACE)
    width = atom_feats.shape[1]
    onehot = (sends[:, None] == jnp.arange(own_count, dtype=jnp.int32)[None, :]).astype(jnp.float32)
    listed = jnp.dot(onehot.astype(atom_feats.dtype), atom_feats, preferred_element_type=jnp.float32)
    spots = jnp.dot(atom_pos, onehot.T, precision=lax.Precision.HIGHEST)
    lanes = -(-(width + 3) // 128) * 128
    both = jnp.concatenate(
        [listed, spots.T, jnp.zeros((listed.shape[0], lanes - width - 3), jnp.float32)], 1
    )
    below, above = exchange(both, 0, ghosts)
    table_feats = jnp.concatenate(
        [atom_feats, below[:, :width].astype(atom_feats.dtype), above[:, :width].astype(atom_feats.dtype)], 0
    )
    table_pos = jnp.concatenate(
        [atom_pos, below[:, width : width + 3].T, above[:, width : width + 3].T], 1
    )
    params = (
        w_zero.astype(jnp.float32),
        w_real.astype(jnp.float32),
        w_imag.astype(jnp.float32),
        radial,
        readout,
    )

    def position_grad(weights):
        return jax.grad(energy, 2)(
            weights, table_feats, table_pos, neighbour_ids, edge_live, shift_list, box_sides
        )

    grad_pos, pullback = jax.vjp(position_grad, params)
    ghost_grad = grad_pos[:, own_count:]
    returned = jnp.concatenate(exchange(ghost_grad, 1, ghosts), 1)
    added = jnp.dot(returned, onehot, precision=lax.Precision.HIGH)
    forces = -(grad_pos[:, :own_count] + added)
    loss_weights = 2.0 * (forces - wanted) / (part_count * own_count)
    picked = jnp.dot(loss_weights, onehot.T, precision=lax.Precision.HIGH)
    table_u = jnp.concatenate([loss_weights, *exchange(picked, 1, ghosts)], 1)
    (grads,) = pullback(-table_u)
    grad_zero, grad_real, grad_imag, grad_radial, grad_readout = all_sum(grads)
    return (forces[None], grad_zero, grad_real, grad_imag, grad_radial, grad_readout)


SPACE = ("zl", "x", "c")
GROUP = ("y", "zh")
STAGES = (("c",), ("x", "y"), ("zh", "zl"))


def all_sum(grads):
    lanes = 128
    blocks = []
    for g in grads:
        g = g.reshape(-1, g.shape[-1]) if g.ndim > 1 else g.reshape(1, -1)
        g = jnp.pad(g, ((0, -g.shape[0] % 16), (0, 0)))
        blocks += [g[:, j : j + lanes] for j in range(0, g.shape[1], lanes)]
    total = sum(b.shape[0] for b in blocks)
    devices = 1
    for stage in STAGES:
        devices *= lax.axis_size(stage)
    rows = -(-total // (devices * 16)) * devices * 16
    blocks.append(jnp.zeros((rows - total, lanes), jnp.float32))
    part = jnp.concatenate(blocks, 0).astype(jnp.bfloat16)
    for stage in STAGES:
        count = lax.axis_size(stage)
        got = lax.all_to_all(part, stage, 0, 0, tiled=True)
        part = got.reshape(count, -1, lanes).astype(jnp.float32).sum(0).astype(jnp.bfloat16)
    for stage in STAGES[::-1]:
        count = lax.axis_size(stage)
        spread = jnp.broadcast_to(part[None], (count,) + part.shape).reshape(-1, lanes)
        part = lax.all_to_all(spread, stage, 0, 0, tiled=True)
    out, start = [], 0
    for g in grads:
        height = g.shape[0] if g.ndim > 1 else 1
        pieces = []
        for _ in range(0, g.shape[-1], lanes):
            pieces.append(part[start : start + height])
            start += height + (-height % 16)
        out.append(jnp.concatenate(pieces, 1).astype(jnp.float32).reshape(g.shape))
    return out


def solution(mesh):
    space, group = mesh.shape["space"], mesh.shape["group"]
    sub = Mesh(
        mesh.devices.reshape(space // 8, 4, 2, group // 2, 2),
        ("zl", "x", "c", "y", "zh"),
    )
    S, G = SPACE, GROUP
    in_specs = (
        P(G, S, None),
        P(G, None, S),
        P(G, None),
        P(G, S),
        P(G, S, None),
        P(G, S, None),
        P(G, S, None),
        P(G, None, S),
        P(),
        P(),
        P(),
        P(),
        P(),
    )
    out_specs = (P(G, None, S), P(), P(), P(), P(), P())
    return jax.shard_map(
        per_device, mesh=sub, in_specs=in_specs, out_specs=out_specs, check_vma=False
    )
```

```python
import jax
import jax.numpy as jnp
from jax import lax
from jax.sharding import Mesh, PartitionSpec as P

RANGE_TOP = 48.0


def exchange(cells, dim, width):
    count = lax.axis_size(SPACE)
    head = lax.slice_in_dim(cells, 0, width, axis=dim)
    tail = lax.slice_in_dim(cells, cells.shape[dim] - width, cells.shape[dim], axis=dim)
    from_below = lax.ppermute(tail, SPACE, [(i, (i + 1) % count) for i in range(count)])
    from_above = lax.ppermute(head, SPACE, [((i + 1) % count, i) for i in range(count)])
    return from_below, from_above


def blocks_matrix(count, width):
    rows = lax.broadcasted_iota(jnp.int32, (count * width, width), 0)
    cols = lax.broadcasted_iota(jnp.int32, (count * width, width), 1)
    return (rows % width == cols).astype(jnp.float32)


def tiled(block, count):
    return jnp.dot(block, blocks_matrix(count, block.shape[1]).T, precision=lax.Precision.HIGH)


def block_sum(wide, width):
    return jnp.dot(wide, blocks_matrix(wide.shape[1] // width, width), precision=lax.Precision.HIGH)


def energy(params, table_feats, table_pos, neighbours, edge_mask, shift_ids, cell_box):
    w_zero, w_real, w_imag, radial, readout = params
    target_count, degree = neighbours.shape
    levels, channels = radial.shape
    flat_ids = neighbours.T.reshape(-1)
    shift_list = shift_ids.T.reshape(-1)
    live = edge_mask.T.reshape(-1)
    offset = (
        jnp.stack([shift_list // 9 - 1, shift_list // 3 % 3 - 1, shift_list % 3 - 1]).astype(
            jnp.float32
        )
        * cell_box[:, None]
    )
    rows = lax.broadcasted_iota(jnp.int32, (table_pos.shape[1], flat_ids.shape[0]), 0)
    select = (rows == flat_ids[None, :]).astype(jnp.float32)
    edge_vec = (
        jnp.dot(table_pos, select, precision=lax.Precision.HIGHEST)
        + offset
        - jnp.concatenate([table_pos[:, :target_count]] * degree, axis=1)
    )
    delta_one, delta_two, delta_three = (edge_vec[0], edge_vec[1], edge_vec[2])
    planar = jnp.sqrt(delta_one * delta_one + delta_two * delta_two + 1.0)
    radius = jnp.sqrt(planar * planar + delta_three * delta_three)
    cos_phi = (delta_one / planar)[:, None]
    sin_phi = (delta_two / planar)[:, None]
    cos_tilt = (delta_three / radius)[:, None]
    sin_tilt = (planar / radius)[:, None]
    spacing = RANGE_TOP / (levels - 1)
    centers = jnp.arange(levels, dtype=jnp.float32) * spacing
    basis_vals = jnp.exp(-jnp.square((radius[:, None] - centers[None, :]) / (2.0 * spacing)))
    radial_gain = jnp.dot(basis_vals, radial, precision=lax.Precision.HIGHEST)
    c = channels
    source = jnp.dot(
        select.T.astype(table_feats.dtype), table_feats, preferred_element_type=jnp.float32
    )
    zero_part = source[:, 0 : 7 * c]
    plus_part = source[:, 7 * c : 13 * c]
    minus_part = source[:, 13 * c : 19 * c]
    plus_turn = cos_phi * plus_part + sin_phi * minus_part
    minus_turn = cos_phi * minus_part - sin_phi * plus_part
    upper = zero_part[:, c:]
    upper_tilt = cos_tilt * upper - sin_tilt * plus_turn
    plus_tilt = sin_tilt * upper + cos_tilt * plus_turn
    gain_six = tiled(radial_gain, 6)
    in_zero = (
        jnp.concatenate([zero_part[:, :c], upper_tilt], 1) * tiled(radial_gain, 7)
    ).astype(jnp.bfloat16)
    in_plus = (plus_tilt * gain_six).astype(jnp.bfloat16)
    in_minus = (minus_turn * gain_six).astype(jnp.bfloat16)
    weight_zero = w_zero.astype(jnp.bfloat16)
    weight_real = w_real.astype(jnp.bfloat16)
    weight_imag = w_imag.astype(jnp.bfloat16)
    out_zero = jnp.dot(in_zero, weight_zero, preferred_element_type=jnp.float32)
    out_plus = jnp.dot(in_plus, weight_real, preferred_element_type=jnp.float32) - jnp.dot(
        in_minus, weight_imag, preferred_element_type=jnp.float32
    )
    out_minus = jnp.dot(in_plus, weight_imag, preferred_element_type=jnp.float32) + jnp.dot(
        in_minus, weight_real, preferred_element_type=jnp.float32
    )
    zero_upper = out_zero[:, c:]
    upper_back = cos_tilt * zero_upper + sin_tilt * out_plus
    plus_back = cos_tilt * out_plus - sin_tilt * zero_upper
    plus_final = cos_phi * plus_back - sin_phi * out_minus
    minus_final = cos_phi * out_minus + sin_phi * plus_back
    message = jnp.concatenate([out_zero[:, :c], upper_back, plus_final, minus_final], 1)
    message = message * live.astype(jnp.float32)[:, None]
    summed = message[:target_count]
    for k in range(1, degree):
        summed = summed + message[k * target_count : (k + 1) * target_count]
    summed = summed / degree
    updated = table_feats[:target_count].astype(jnp.float32) + summed
    square = updated * updated
    total = block_sum(square, c)
    invariant = updated[:, :c] + total / 19
    return jnp.sum(jax.nn.silu(invariant) * readout[None, :])


def per_device(
    features,
    positions,
    cell_box,
    send_rows,
    neighbours,
    edge_mask,
    shift_ids,
    target_forces,
    w_zero,
    w_real,
    w_imag,
    radial,
    readout,
):
    atom_feats = features[0]
    atom_pos = positions[0]
    box_sides = cell_box[0]
    sends = send_rows[0]
    neighbour_ids = neighbours[0]
    edge_live = edge_mask[0]
    shift_list = shift_ids[0]
    wanted = target_forces[0]
    own_count = atom_feats.shape[0]
    ghosts = sends.shape[0] // 2
    part_count = lax.axis_size(SPACE)
    width = atom_feats.shape[1]
    onehot = (sends[:, None] == jnp.arange(own_count, dtype=jnp.int32)[None, :]).astype(jnp.float32)
    listed = jnp.dot(onehot.astype(atom_feats.dtype), atom_feats, preferred_element_type=jnp.float32)
    spots = jnp.dot(atom_pos, onehot.T, precision=lax.Precision.HIGHEST)
    lanes = -(-(width + 3) // 128) * 128
    both = jnp.concatenate(
        [listed, spots.T, jnp.zeros((listed.shape[0], lanes - width - 3), jnp.float32)], 1
    )
    below, above = exchange(both, 0, ghosts)
    table_feats = jnp.concatenate(
        [atom_feats, below[:, :width].astype(atom_feats.dtype), above[:, :width].astype(atom_feats.dtype)], 0
    )
    table_pos = jnp.concatenate(
        [atom_pos, below[:, width : width + 3].T, above[:, width : width + 3].T], 1
    )
    params = (
        w_zero.astype(jnp.float32),
        w_real.astype(jnp.float32),
        w_imag.astype(jnp.float32),
        radial,
        readout,
    )

    def position_grad(weights):
        return jax.grad(energy, 2)(
            weights, table_feats, table_pos, neighbour_ids, edge_live, shift_list, box_sides
        )

    grad_pos, pullback = jax.vjp(position_grad, params)
    ghost_grad = grad_pos[:, own_count:]
    returned = jnp.concatenate(exchange(ghost_grad, 1, ghosts), 1)
    added = jnp.dot(returned, onehot, precision=lax.Precision.HIGHEST)
    forces = -(grad_pos[:, :own_count] + added)
    loss_weights = 2.0 * (forces - wanted) / (part_count * own_count)
    picked = jnp.dot(loss_weights, onehot.T, precision=lax.Precision.HIGHEST)
    table_u = jnp.concatenate([loss_weights, *exchange(picked, 1, ghosts)], 1)
    (grads,) = pullback(-table_u)
    grad_zero, grad_real, grad_imag, grad_radial, grad_readout = all_sum(grads)
    return (forces[None], grad_zero, grad_real, grad_imag, grad_radial, grad_readout)


SPACE = ("zl", "x", "c")
GROUP = ("y", "zh")
STAGES = (("c",), ("x", "y"), ("zh", "zl"))


def all_sum(grads):
    lanes = 128
    blocks = []
    for g in grads:
        g = g.reshape(-1, g.shape[-1]) if g.ndim > 1 else g.reshape(1, -1)
        g = jnp.pad(g, ((0, -g.shape[0] % 16), (0, 0)))
        blocks += [g[:, j : j + lanes] for j in range(0, g.shape[1], lanes)]
    total = sum(b.shape[0] for b in blocks)
    devices = 1
    for stage in STAGES:
        devices *= lax.axis_size(stage)
    rows = -(-total // devices) * devices
    blocks.append(jnp.zeros((rows - total, lanes), jnp.float32))
    part = jnp.concatenate(blocks, 0).astype(jnp.bfloat16)
    for stage in STAGES:
        count = lax.axis_size(stage)
        got = lax.all_to_all(part, stage, 0, 0, tiled=True)
        part = got.reshape(count, -1, lanes).astype(jnp.float32).sum(0).astype(jnp.bfloat16)
    for stage in STAGES[::-1]:
        count = lax.axis_size(stage)
        spread = jnp.broadcast_to(part[None], (count,) + part.shape).reshape(-1, lanes)
        part = lax.all_to_all(spread, stage, 0, 0, tiled=True)
    out, start = [], 0
    for g in grads:
        height = g.shape[0] if g.ndim > 1 else 1
        pieces = []
        for _ in range(0, g.shape[-1], lanes):
            pieces.append(part[start : start + height])
            start += height + (-height % 16)
        out.append(jnp.concatenate(pieces, 1).astype(jnp.float32).reshape(g.shape))
    return out


def solution(mesh):
    space, group = mesh.shape["space"], mesh.shape["group"]
    sub = Mesh(
        mesh.devices.reshape(space // 8, 4, 2, group // 2, 2),
        ("zl", "x", "c", "y", "zh"),
    )
    S, G = SPACE, GROUP
    in_specs = (
        P(G, S, None),
        P(G, None, S),
        P(G, None),
        P(G, S),
        P(G, S, None),
        P(G, S, None),
        P(G, S, None),
        P(G, None, S),
        P(),
        P(),
        P(),
        P(),
        P(),
    )
    out_specs = (P(G, None, S), P(), P(), P(), P(), P())
    return jax.shard_map(
        per_device, mesh=sub, in_specs=in_specs, out_specs=out_specs, check_vma=False
    )
```
